512 devices in a mesh: seq: 16 (over z, y_lo), wt: 32 (over x, y_hi, core).
Axes of the slice: x: 4, y: 8 (y_hi: 4, y_lo: 2; y = y_hi * 2 + y_lo), z: 8, core: 2. Of those that a mesh axis runs over, the one named last changes fastest.
Arguments:
- tokens_in: bfloat16 [3584, 4608], P('seq', 'wt'), may hold values from -6 to 6
- norm_gain: float32 [4608], P('wt'), may hold values from 0.25 to 1.75
- positions: int32 [3584], P('seq'), may hold values from 0 to 2687, as said below
- blocks: bfloat16 [32, 64, 128, 128], P('wt'), may hold values from -0.125 to 0.125
- slot_code: int32 [32, 64], P('wt'), may hold values from -1 to 2303, as said below
- out_grad: bfloat16 [3584, 4096], P('seq', 'wt'), may hold values from -6 to 6
Outputs:
- attn_out: bfloat16 [3584, 4096], P('seq', 'wt')
- tokens_grad: bfloat16 [3584, 4608], P('seq', 'wt')
- gain_grad: float32 [4608], P('wt')
- block_grads: bfloat16 [32, 64, 128, 128], P('wt')
The draws below stay inside these ranges and needn't reach their ends.
Inputs may be any that keep to these rules, and one draw needn't show every extreme that they name: Positions count the tokens of each document from 0: positions[0] = 0 and every later entry is either 0 (a new document starts) or the entry before plus one. The longest document has exactly 2688 tokens. slot_code[o, s] is -1 for an empty slot, else u * 2 * 36 + p with head u and 0 <= p < 72; no value other than -1 appears twice. One owner holds at most 2 blocks for one head; in every draw some owner holds 2 blocks for every head and some head has 2 blocks at every owner.
All inputs are finite; a program needn't handle non-finite values.
Results may differ from the reference program's by a relative error of at most 0.023.
Values may be sent and summed in bfloat16 or wider, within the bound.
No kernel may reach another device: no remote copies, remote signals or barrier semaphores. Data moves between devices by JAX's collectives and lax.ppermute only.
A program may use at most 64 MiB of HBM per device.

```python
from functools import partial
import jax
import jax.numpy as jnp
from jax import lax

D = 4608
HD = 128
BLK = 128
CAP = 2
TOK_DEV = 224
HEADS = 32
RB = 36
SLOTS = 64
TOKENS = 3584
WINDOW = 1792
N_SEQ = 16
N_WT = 32


def order_of(sub_key, count):
    order = jax.random.permutation(sub_key, count)
    index = jnp.arange(count, dtype=jnp.int32)
    last_value = count - 1
    return jnp.where(index == 0, last_value, jnp.where(order == last_value, order[0], order))


def draw_slot_code(key, part):
    sub_keys = jax.random.split(key, 5)
    groups = N_WT
    pos_count = 2 * (D // BLK)
    counts = jax.random.randint(sub_keys[0], (groups, groups), 0, CAP + 1)
    full_owner = jax.random.randint(sub_keys[1], (), 0, groups)
    full_user = jax.random.randint(sub_keys[2], (), 0, groups)
    owner_ids = jnp.arange(groups, dtype=jnp.int32)[:, None]
    user_ids = jnp.arange(groups, dtype=jnp.int32)[None, :]
    forced = (owner_ids == full_owner) | (user_ids == full_user) | (owner_ids == 0) & (user_ids == groups - 1)
    counts = jnp.where(forced, CAP, counts)
    earlier = jnp.cumsum(counts, axis=0) - counts
    orders = jax.vmap(partial(order_of, count=pos_count))(jax.random.split(sub_keys[3], groups))
    within = jnp.arange(CAP, dtype=jnp.int32)[None, None, :]
    pick_index = jnp.minimum(earlier[:, :, None] + within, pos_count - 1)
    chosen = jnp.take_along_axis(jnp.broadcast_to(orders[None], (groups, groups, pos_count)), pick_index, axis=2)
    is_live = within < counts[:, :, None]
    codes = jnp.where(is_live, user_ids[:, :, None] * pos_count + chosen, -1).reshape(groups, groups * CAP)
    shuffle = jax.vmap(jax.random.permutation, in_axes=(0, None))(jax.random.split(sub_keys[4], groups), groups * CAP)
    return jnp.take_along_axis(codes, shuffle, axis=1).astype(jnp.int32)


def draw_positions(key, part):
    sub_keys = jax.random.split(key, 2)
    long_doc = 3 * TOKENS // 4
    long_start = jax.random.randint(sub_keys[0], (), 0, TOKENS - long_doc + 1)
    extra_cut = jax.random.randint(sub_keys[1], (), 1, TOKENS)
    extra_ok = (extra_cut <= long_start) | (extra_cut >= long_start + long_doc)
    token_index = jnp.arange(TOKENS, dtype=jnp.int32)
    is_start = (token_index == 0) | (token_index == long_start) | (token_index == long_start + long_doc) | (token_index == extra_cut) & extra_ok
    starts = jnp.where(is_start, token_index, 0)
    return (token_index - lax.cummax(starts, axis=0)).astype(jnp.int32)


def block_scale(key, shape, pieces, low, largest):
    loudness = 1.0
    for position, shards_of in pieces:
        heights = jax.random.uniform(jax.random.fold_in(jax.random.fold_in(key, 6), position), (shards_of,), jnp.float32, low / len(pieces), largest / len(pieces))
        loudness = loudness * jnp.repeat(jnp.exp(heights), shape[position] // shards_of).reshape((-1,) + (1,) * (len(shape) - 1 - position))
    return loudness


def noise(rng, shape, spread, reach, cuts=(), kind=jnp.bfloat16):
    array = jax.random.normal(rng, shape, jnp.float32) * spread
    if len(cuts) > 0:
        array = block_scale(rng, shape, cuts, -0.22, 0.18) * array
    return jnp.clip(array, min=-reach, max=reach).astype(kind)


def setup_inputs(seed: int = 0) -> dict:
    seeds = jax.random.split(jax.random.key(seed), 7)
    tokens_in = noise(seeds[0], (TOKENS, D), 1.0, 6.0, ((0, 16), (1, 32)))
    norm_gain = jnp.clip(1.0 + 0.15 * jax.random.normal(seeds[1], (D,), jnp.float32), 0.25, 1.75)
    positions = draw_positions(jax.random.fold_in(seeds[6], 71), 0)
    blocks = noise(seeds[3], (N_WT, SLOTS, BLK, BLK), (D // 2) ** -0.5, 0.125, ((0, 32),))
    slot_code = draw_slot_code(jax.random.fold_in(seeds[6], 71), 0)
    out_grad = noise(seeds[5], (TOKENS, HEADS * HD), 1.0, 6.0, ((0, 16), (1, 32)))
    return {"tokens_in": tokens_in, "norm_gain": norm_gain, "positions": positions, "blocks": blocks, "slot_code": slot_code, "out_grad": out_grad}


query_scale = 144.0 ** (-0.5)
soft_cap = 50.0
norm_eps = 1e-06

def rounded(values):
    return lax.optimization_barrier(values.astype(jnp.bfloat16)).astype(jnp.float32)

def rope_tables(positions, head_width):
    half_width = head_width // 2
    frequency = 10000.0 ** (-2.0 * jnp.arange(half_width, dtype=jnp.float32) / head_width)
    angles = positions.astype(jnp.float32)[:, None] * frequency[None, :]
    return (jnp.cos(angles), jnp.sin(angles))

def rotate(vector, cos_table, sin_table):
    half_width = vector.shape[-1] // 2
    first_half = vector[..., :half_width]
    second_half = vector[..., half_width:]
    return jnp.concatenate([first_half * cos_table - second_half * sin_table, first_half * sin_table + second_half * cos_table], axis=-1)

def reference(tokens_in, norm_gain, positions, blocks, slot_code, out_grad):
    tokens_f32 = tokens_in.astype(jnp.float32)
    inv_rms = lax.rsqrt(lax.optimization_barrier(jnp.mean(tokens_f32 * tokens_f32, axis=1)) + norm_eps)
    scaled = tokens_f32 * inv_rms[:, None]
    normed = (scaled * norm_gain[None, :]).astype(jnp.bfloat16)
    normed_f32 = normed.astype(jnp.float32)
    slab_normed = normed_f32.reshape(N_SEQ, TOK_DEV, D)
    pos_total = HEADS * 2 * RB
    slot_codes = slot_code.reshape(-1)
    flat_blocks = blocks.reshape(-1, BLK, BLK)
    block_target = jnp.where(slot_codes < 0, pos_total, slot_codes).astype(jnp.int32)
    weight_table = jnp.zeros((pos_total + 1, BLK, BLK), jnp.bfloat16).at[block_target].set(flat_blocks)
    weight_table = weight_table[:pos_total].reshape(HEADS, 2, D, HD)
    cos_table, sin_table = rope_tables(positions, HD)
    token_index = jnp.arange(TOKENS, dtype=jnp.int32)
    doc_begin = token_index - positions
    distance = token_index[:, None] - token_index[None, :]
    visible = (distance >= 0) & (distance < WINDOW) & (token_index[None, :] >= doc_begin[:, None])
    out_heads = out_grad.reshape(TOKENS, HEADS, HD).transpose(1, 0, 2)

    def group(normed_grad, group_index):
        first_head = (2 * group_index).astype(jnp.int32)
        pair_weights = lax.dynamic_slice_in_dim(weight_table, first_head, 2, 0)
        w_query = pair_weights[:, 0]
        w_key = pair_weights[0, 1]
        w_value = pair_weights[1, 1]
        query_proj = jnp.einsum('td,hdf->htf', normed_f32, w_query.astype(jnp.float32))
        key_proj = jnp.dot(normed, w_key, preferred_element_type=jnp.float32)
        value_proj = jnp.dot(normed, w_value, preferred_element_type=jnp.float32)
        query_rot = (rotate(query_proj, cos_table, sin_table) * query_scale).astype(jnp.bfloat16).astype(jnp.float32)
        key_rot = rotate(key_proj, cos_table, sin_table).astype(jnp.bfloat16).astype(jnp.float32)
        value_low = value_proj.astype(jnp.bfloat16).astype(jnp.float32)
        scores = jnp.einsum('htf,sf->hts', query_rot, key_rot)
        capped = soft_cap * jnp.tanh(scores / soft_cap)
        exp_scores = jnp.where(visible[None], jnp.exp(capped), 0.0)
        row_total = lax.optimization_barrier(jnp.sum(exp_scores, axis=2))
        head_out = (jnp.einsum('hts,sf->htf', rounded(exp_scores), value_low) / row_total[:, :, None]).astype(jnp.bfloat16)
        out_slice = lax.dynamic_slice_in_dim(out_heads, first_head, 2, 0).astype(jnp.float32)
        row_delta = lax.optimization_barrier(jnp.sum(out_slice * head_out.astype(jnp.float32), axis=2))
        soft_probs = exp_scores / row_total[:, :, None]
        prob_grad = jnp.einsum('htf,sf->hts', out_slice, value_low)
        score_grad = soft_probs * (prob_grad - row_delta[:, :, None]) * (1.0 - (capped / soft_cap) ** 2)
        score_low = rounded(score_grad)
        probs_low = rounded(soft_probs)
        rot_grad = jnp.einsum('hts,sf->htf', score_low, key_rot)
        query_grad = (rotate(rot_grad, cos_table, -sin_table) * query_scale).astype(jnp.bfloat16)
        key_rot_grad = jnp.einsum('hts,htf->sf', score_low, query_rot)
        key_grad = rotate(key_rot_grad, cos_table, -sin_table).astype(jnp.bfloat16)
        value_grad = jnp.einsum('hts,htf->sf', probs_low, out_slice).astype(jnp.bfloat16)
        normed_grad = normed_grad + jnp.einsum('htf,hdf->td', query_grad.astype(jnp.float32), w_query.astype(jnp.float32))
        normed_grad = normed_grad + jnp.dot(key_grad, w_key.T, preferred_element_type=jnp.float32)
        normed_grad = normed_grad + jnp.dot(value_grad, w_value.T, preferred_element_type=jnp.float32)
        cotangents = jnp.stack([query_grad[0], key_grad, query_grad[1], value_grad]).astype(jnp.float32)
        per_slab = jnp.einsum('std,cstf->csdf', slab_normed, cotangents.reshape(4, N_SEQ, TOK_DEV, HD))
        weight_grads = lax.optimization_barrier(jnp.sum(rounded(per_slab), axis=1)).astype(jnp.bfloat16)
        return (normed_grad, (head_out, weight_grads))
    normed_grad, (head_out, weight_grads) = lax.scan(group, jnp.zeros((TOKENS, D), jnp.float32), jnp.arange(HEADS // 2, dtype=jnp.int32))
    attn_out = head_out.reshape(HEADS, TOKENS, HD).transpose(1, 0, 2).reshape(TOKENS, HEADS * HD)
    grad_table = weight_grads.reshape(HEADS * 2 * RB, BLK, BLK)
    padded = jnp.concatenate([grad_table, jnp.zeros((1, BLK, BLK), jnp.bfloat16)], axis=0)
    block_grads = padded[block_target].reshape(N_WT, SLOTS, BLK, BLK)
    scaled_grad = normed_grad * norm_gain[None, :]
    mean_prod = lax.optimization_barrier(jnp.mean(scaled_grad * scaled, axis=1))
    tokens_grad = (inv_rms[:, None] * (scaled_grad - scaled * mean_prod[:, None])).astype(jnp.bfloat16)
    gain_slab = lax.optimization_barrier(jnp.sum((normed_grad * scaled).reshape(N_SEQ, TOK_DEV, D), axis=1))
    gain_grad = lax.optimization_barrier(jnp.sum(rounded(gain_slab), axis=0))
    return (attn_out, tokens_grad, gain_grad, block_grads)
```

```python
import jax
import jax.numpy as jnp
from jax import lax
from jax.sharding import PartitionSpec as P

D = 4608
HD = 128
BLK = 128
CAP = 2


query_scale = 144.0 ** (-0.5)
soft_cap = 50.0
norm_eps = 1e-06


def from_partner(block, axis, stride):
    count = lax.axis_size(axis)
    route = []
    for low in range(count):
        high = low | 1 << stride
        if high != low and high < count:
            route += [(low, high), (high, low)]
    return lax.ppermute(block, axis, route)


def shifted(value, axis, steps):
    count = lax.axis_size(axis)
    initial, last = (max(0, -steps), min(count, count - steps))
    return lax.ppermute(value, axis, [(source, source + steps) for source in range(initial, last)])


def rope_tables(positions, head_width):
    half_width = head_width // 2
    frequency = 10000.0 ** (-2.0 * jnp.arange(half_width, dtype=jnp.float32) / head_width)
    angles = positions.astype(jnp.float32)[:, None] * frequency[None, :]
    return (jnp.cos(angles), jnp.sin(angles))


def rotate(vector, cos_table, sin_table):
    half_width = vector.shape[-1] // 2
    first_half = vector[..., :half_width]
    second_half = vector[..., half_width:]
    return jnp.concatenate(
        [
            first_half * cos_table - second_half * sin_table,
            first_half * sin_table + second_half * cos_table,
        ],
        axis=-1,
    )


def contract(left, right):
    return lax.dot_general(
        left, right, (((1,), (1,)), ((), ())), preferred_element_type=jnp.float32
    )


def contract_rows(left, right):
    return lax.dot_general(
        left, right, (((0,), (0,)), ((), ())), preferred_element_type=jnp.float32
    )


def body(tokens_in, norm_gain, positions, blocks, slot_code, out_grad):
    tok_rows = tokens_in.shape[0]
    feat = tokens_in.shape[1]
    groups = lax.axis_size("wt")
    slab_index = lax.axis_index("seq")
    is_even = lax.axis_index("wt") % 2 == 0
    pos_count = 2 * (D // BLK)
    row_blocks = pos_count // 2
    slot_codes = slot_code[0]
    is_live = slot_codes >= 0
    target_user = jnp.where(is_live, slot_codes // pos_count, 0)
    user_match = (
        (target_user[:, None] == jnp.arange(groups, dtype=jnp.int32)[None, :]) & is_live[:, None]
    ).astype(jnp.int32)
    earlier = jnp.cumsum(user_match, axis=0) - user_match
    slot_rank = jnp.sum(earlier * user_match, axis=1)
    dump_slot = groups * CAP
    slot_dest = jnp.where(is_live, target_user * CAP + slot_rank, dump_slot)
    block_place = (slot_codes - target_user * pos_count).astype(jnp.float32)
    outgoing = jnp.zeros((dump_slot + 1, BLK, BLK), jnp.bfloat16).at[slot_dest].set(blocks[0])
    outgoing_pos = (
        jnp.full((dump_slot + 1,), -1.0, jnp.float32)
        .at[slot_dest]
        .set(block_place)
        .astype(jnp.bfloat16)
    )
    arrived, arrived_pos = (
        lax.all_to_all(
            outgoing[:dump_slot].reshape(groups, CAP, BLK, BLK),
            "wt",
            split_axis=0,
            concat_axis=0,
            tiled=True,
        ),
        lax.all_to_all(
            outgoing_pos[:dump_slot].reshape(groups, CAP),
            "wt",
            split_axis=0,
            concat_axis=0,
            tiled=True,
        ),
    )
    gain_hi = lax.reduce_precision(norm_gain, exponent_bits=8, mantissa_bits=7)
    gain_rest = norm_gain - gain_hi
    gain_mid = lax.reduce_precision(gain_rest, exponent_bits=8, mantissa_bits=7)
    gain_lo = gain_rest - gain_mid
    gain_rows = jnp.stack([gain_hi, gain_mid, gain_lo]).astype(jnp.bfloat16)
    side_rows = 8
    gathered = lax.all_gather(
        jnp.concatenate(
            [tokens_in, gain_rows, jnp.zeros((side_rows - 3, feat), jnp.bfloat16)], axis=0
        ),
        "wt",
        axis=1,
        tiled=True,
    )
    tokens_full = gathered[:tok_rows]
    gain_parts = gathered[tok_rows : tok_rows + 3].astype(jnp.float32)
    gain_full = (gain_parts[0] + gain_parts[1]) + gain_parts[2]
    full_f32 = tokens_full.astype(jnp.float32)
    squares = jnp.sum(full_f32 * full_f32, axis=1)
    inv_rms = lax.rsqrt(squares / D + norm_eps)
    scaled_full = full_f32 * inv_rms[:, None]
    gained_full = scaled_full * gain_full[None, :]
    normed = gained_full.astype(jnp.bfloat16)
    scaled = tokens_in.astype(jnp.float32) * inv_rms[:, None]
    arrival = arrived_pos.reshape(-1).astype(jnp.int32)
    arrival = jnp.where(arrival < 0, pos_count, arrival)
    weight_table = (
        jnp.zeros((pos_count + 1, BLK, BLK), jnp.bfloat16)
        .at[arrival]
        .set(arrived.reshape(-1, BLK, BLK))
    )
    w_query = weight_table[:row_blocks].reshape(D, HD)
    w_pair = weight_table[row_blocks:pos_count].reshape(D, HD)
    query_proj = jnp.dot(normed, w_query, preferred_element_type=jnp.float32)
    pair_proj = jnp.dot(normed, w_pair, preferred_element_type=jnp.float32)
    cos_table, sin_table = rope_tables(positions, HD)
    query_rot = (rotate(query_proj, cos_table, sin_table) * query_scale).astype(jnp.bfloat16)
    own_pair = jnp.where(is_even, rotate(pair_proj, cos_table, sin_table), pair_proj).astype(
        jnp.bfloat16
    )
    partner = from_partner(own_pair, "wt", 0)
    key_rows = jnp.where(is_even, own_pair, partner)
    value_rows = jnp.where(is_even, partner, own_pair)
    reach_slabs = lax.axis_size("seq") // 2
    window = reach_slabs * tok_rows
    key_value = jnp.concatenate([key_rows, value_rows], axis=1)
    key_list = [key_rows]
    value_list = [value_rows]
    for offset in range(1, reach_slabs + 1):
        prev = shifted(key_value, "seq", offset)
        key_list.append(prev[:, :HD])
        value_list.append(prev[:, HD:])
    key_all = jnp.concatenate(key_list, axis=0)
    value_all = jnp.concatenate(value_list, axis=0)
    local_index = jnp.arange(tok_rows, dtype=jnp.int32)
    query_index = slab_index * tok_rows + local_index
    key_index = jnp.concatenate(
        [(slab_index - offset) * tok_rows + local_index for offset in range(reach_slabs + 1)]
    )
    doc_begin = query_index - positions
    distance = query_index[:, None] - key_index[None, :]
    visible = (distance >= 0) & (distance < window) & (key_index[None, :] >= doc_begin[:, None])
    scores = contract(query_rot, key_all)
    capped = soft_cap * jnp.tanh(scores / soft_cap)
    exp_scores = jnp.where(visible, jnp.exp(capped), 0.0)
    row_total = jnp.sum(exp_scores, axis=1)
    attn_rows = (
        jnp.dot(exp_scores.astype(jnp.bfloat16), value_all, preferred_element_type=jnp.float32)
        / row_total[:, None]
    ).astype(jnp.bfloat16)
    row_delta = jnp.sum(out_grad.astype(jnp.float32) * attn_rows.astype(jnp.float32), axis=1)
    soft_probs = exp_scores / row_total[:, None]
    prob_grad = contract(out_grad, value_all)
    score_grad = soft_probs * (prob_grad - row_delta[:, None]) * (1.0 - (capped / soft_cap) ** 2)
    score_low = score_grad.astype(jnp.bfloat16)
    probs_low = soft_probs.astype(jnp.bfloat16)
    rot_grad = jnp.dot(score_low, key_all, preferred_element_type=jnp.float32)
    query_grad = (rotate(rot_grad, cos_table, -sin_table) * query_scale).astype(jnp.bfloat16)
    key_grads = contract_rows(score_low, query_rot)
    value_grads = contract_rows(probs_low, out_grad)
    key_total = key_grads[:tok_rows]
    value_total = value_grads[:tok_rows]
    for offset in range(1, reach_slabs + 1):
        piece = jnp.concatenate(
            [
                key_grads[offset * tok_rows : (offset + 1) * tok_rows].astype(jnp.bfloat16),
                value_grads[offset * tok_rows : (offset + 1) * tok_rows].astype(jnp.bfloat16),
            ],
            axis=1,
        )
        recv = shifted(piece, "seq", -offset).astype(jnp.float32)
        key_total = key_total + recv[:, :HD]
        value_total = value_total + recv[:, HD:]
    outbound = jnp.where(is_even, value_total, key_total)
    partner_grad = from_partner(outbound.astype(jnp.bfloat16), "wt", 0).astype(outbound.dtype)
    pair_total = jnp.where(is_even, key_total, value_total) + partner_grad
    pair_grad = jnp.where(is_even, rotate(pair_total, cos_table, -sin_table), pair_total).astype(
        jnp.bfloat16
    )
    contribution = contract(w_query, query_grad) + contract(w_pair, pair_grad)
    row_part = jnp.sum(contribution * gained_full.T, axis=0)
    row_top = lax.reduce_precision(row_part, exponent_bits=8, mantissa_bits=7)
    row_hi = row_top.astype(jnp.bfloat16)
    row_lo = (row_part - row_top).astype(jnp.bfloat16)
    pad_rows = 16
    extra_rows = jnp.concatenate(
        [row_hi[None], row_lo[None], jnp.zeros((pad_rows - 2, tok_rows), jnp.bfloat16)], axis=0
    )
    packed = jnp.concatenate(
        [
            contribution.astype(jnp.bfloat16).reshape(groups, feat, tok_rows),
            jnp.broadcast_to(extra_rows[None], (groups, pad_rows, tok_rows)),
        ],
        axis=1,
    ).reshape(groups * (feat + pad_rows), tok_rows)
    scattered = lax.psum_scatter(packed, "wt", scatter_dimension=0, tiled=True)
    normed_grad = scattered[:feat].astype(jnp.float32).T
    row_dots = scattered[feat].astype(jnp.float32) + scattered[feat + 1].astype(jnp.float32)
    scaled_grad = normed_grad * norm_gain[None, :]
    tokens_grad = (inv_rms[:, None] * (scaled_grad - scaled * (row_dots / D)[:, None])).astype(
        jnp.bfloat16
    )
    gain_part = jnp.sum(normed_grad * scaled, axis=0)
    grad_query = contract_rows(normed, query_grad)
    grad_pair = contract_rows(normed, pair_grad)
    grad_table = jnp.concatenate(
        [
            grad_query.reshape(row_blocks, BLK, BLK),
            grad_pair.reshape(row_blocks, BLK, BLK),
            jnp.zeros((1, BLK, BLK), jnp.float32),
        ],
        axis=0,
    )
    slot_grads = grad_table[arrival].reshape(groups, CAP, BLK, BLK)
    empty_block = jnp.zeros((1, BLK, BLK), jnp.bfloat16)
    returned = lax.all_to_all(
        slot_grads.astype(jnp.bfloat16), "wt", split_axis=0, concat_axis=0, tiled=True
    )
    owned_grads = jnp.concatenate([returned.reshape(-1, BLK, BLK), empty_block], axis=0)[slot_dest]
    gain_block = jnp.pad(gain_part.astype(jnp.bfloat16), (0, BLK * BLK - feat)).reshape(1, BLK, BLK)
    summed = lax.psum(jnp.concatenate([owned_grads, gain_block], axis=0), "seq")
    block_grads = summed[:-1]
    gain_total = summed[-1].reshape(-1)[:feat].astype(jnp.float32)
    return (attn_rows, tokens_grad, gain_total, block_grads[None])


def solution(mesh):
    placed = (
        P("seq", "wt"),
        P("wt"),
        P("seq"),
        P("wt", None, None, None),
        P("wt", None),
        P("seq", "wt"),
    )
    return jax.shard_map(
        body,
        mesh=mesh,
        in_specs=placed,
        out_specs=(P("seq", "wt"), P("seq", "wt"), P("wt"), P("wt", None, None, None)),
        check_vma=False,
    )
```

```python
import jax
import jax.numpy as jnp
from jax import lax
from jax.sharding import PartitionSpec as P

D = 4608
HD = 128
BLK = 128
CAP = 2


query_scale = 144.0 ** (-0.5)
soft_cap = 50.0
norm_eps = 1e-06


def from_partner(block, axis, stride):
    count = lax.axis_size(axis)
    route = []
    for low in range(count):
        high = low | 1 << stride
        if high != low and high < count:
            route += [(low, high), (high, low)]
    return lax.ppermute(block, axis, route)


def shifted(value, axis, steps):
    count = lax.axis_size(axis)
    initial, last = (max(0, -steps), min(count, count - steps))
    return lax.ppermute(value, axis, [(source, source + steps) for source in range(initial, last)])


def rope_tables(positions, head_width):
    half_width = head_width // 2
    frequency = 10000.0 ** (-2.0 * jnp.arange(half_width, dtype=jnp.float32) / head_width)
    angles = positions.astype(jnp.float32)[:, None] * frequency[None, :]
    return (jnp.cos(angles), jnp.sin(angles))


def rotate(vector, cos_table, sin_table):
    half_width = vector.shape[-1] // 2
    first_half = vector[..., :half_width]
    second_half = vector[..., half_width:]
    return jnp.concatenate(
        [
            first_half * cos_table - second_half * sin_table,
            first_half * sin_table + second_half * cos_table,
        ],
        axis=-1,
    )


def contract(left, right):
    return lax.dot_general(
        left, right, (((1,), (1,)), ((), ())), preferred_element_type=jnp.float32
    )


def contract_rows(left, right):
    return lax.dot_general(
        left, right, (((0,), (0,)), ((), ())), preferred_element_type=jnp.float32
    )


def body(tokens_in, norm_gain, positions, blocks, slot_code, out_grad):
    tok_rows = tokens_in.shape[0]
    feat = tokens_in.shape[1]
    groups = lax.axis_size("wt")
    slab_index = lax.axis_index("seq")
    is_even = lax.axis_index("wt") % 2 == 0
    pos_count = 2 * (D // BLK)
    row_blocks = pos_count // 2
    slot_codes = slot_code[0]
    is_live = slot_codes >= 0
    target_user = jnp.where(is_live, slot_codes // pos_count, 0)
    user_match = (
        (target_user[:, None] == jnp.arange(groups, dtype=jnp.int32)[None, :]) & is_live[:, None]
    ).astype(jnp.int32)
    earlier = jnp.cumsum(user_match, axis=0) - user_match
    slot_rank = jnp.sum(earlier * user_match, axis=1)
    dump_slot = groups * CAP
    slot_dest = jnp.where(is_live, target_user * CAP + slot_rank, dump_slot)
    block_place = (slot_codes - target_user * pos_count).astype(jnp.float32)
    outgoing = jnp.zeros((dump_slot + 1, BLK, BLK), jnp.bfloat16).at[slot_dest].set(blocks[0])
    outgoing_pos = (
        jnp.full((dump_slot + 1,), -1.0, jnp.float32)
        .at[slot_dest]
        .set(block_place)
        .astype(jnp.bfloat16)
    )
    arrived, arrived_pos = (
        lax.all_to_all(
            outgoing[:dump_slot].reshape(groups, CAP, BLK, BLK),
            "wt",
            split_axis=0,
            concat_axis=0,
            tiled=True,
        ),
        lax.all_to_all(
            outgoing_pos[:dump_slot].reshape(groups, CAP),
            "wt",
            split_axis=0,
            concat_axis=0,
            tiled=True,
        ),
    )
    gain_hi = lax.reduce_precision(norm_gain, exponent_bits=8, mantissa_bits=7)
    gain_rest = norm_gain - gain_hi
    gain_mid = lax.reduce_precision(gain_rest, exponent_bits=8, mantissa_bits=7)
    gain_lo = gain_rest - gain_mid
    gain_rows = jnp.stack([gain_hi, gain_mid, gain_lo]).astype(jnp.bfloat16)
    side_rows = 8
    gathered = lax.all_gather(
        jnp.concatenate(
            [tokens_in, gain_rows, jnp.zeros((side_rows - 3, feat), jnp.bfloat16)], axis=0
        ),
        "wt",
        axis=1,
        tiled=True,
    )
    tokens_full = gathered[:tok_rows]
    gain_parts = gathered[tok_rows : tok_rows + 3].astype(jnp.float32)
    gain_full = (gain_parts[0] + gain_parts[1]) + gain_parts[2]
    full_f32 = tokens_full.astype(jnp.float32)
    squares = jnp.sum(full_f32 * full_f32, axis=1)
    inv_rms = lax.rsqrt(squares / D + norm_eps)
    scaled_full = full_f32 * inv_rms[:, None]
    gained_full = scaled_full * gain_full[None, :]
    normed = gained_full.astype(jnp.bfloat16)
    scaled = tokens_in.astype(jnp.float32) * inv_rms[:, None]
    arrival = arrived_pos.reshape(-1).astype(jnp.int32)
    arrival = jnp.where(arrival < 0, pos_count, arrival)
    weight_table = (
        jnp.zeros((pos_count + 1, BLK, BLK), jnp.bfloat16)
        .at[arrival]
        .set(arrived.reshape(-1, BLK, BLK))
    )
    w_query = weight_table[:row_blocks].reshape(D, HD)
    w_pair = weight_table[row_blocks:pos_count].reshape(D, HD)
    query_proj = jnp.dot(normed, w_query, preferred_element_type=jnp.float32)
    pair_proj = jnp.dot(normed, w_pair, preferred_element_type=jnp.float32)
    cos_table, sin_table = rope_tables(positions, HD)
    query_rot = (rotate(query_proj, cos_table, sin_table) * query_scale).astype(jnp.bfloat16)
    own_pair = jnp.where(is_even, rotate(pair_proj, cos_table, sin_table), pair_proj).astype(
        jnp.bfloat16
    )
    partner = from_partner(own_pair, "wt", 0)
    key_rows = jnp.where(is_even, own_pair, partner)
    value_rows = jnp.where(is_even, partner, own_pair)
    reach_slabs = lax.axis_size("seq") // 2
    window = reach_slabs * tok_rows
    key_value = jnp.concatenate([key_rows, value_rows], axis=1)
    key_list = [key_rows]
    value_list = [value_rows]
    for offset in range(1, reach_slabs + 1):
        prev = shifted(key_value, "seq", offset)
        key_list.append(prev[:, :HD])
        value_list.append(prev[:, HD:])
    key_all = jnp.concatenate(key_list, axis=0)
    value_all = jnp.concatenate(value_list, axis=0)
    local_index = jnp.arange(tok_rows, dtype=jnp.int32)
    query_index = slab_index * tok_rows + local_index
    key_index = jnp.concatenate(
        [(slab_index - offset) * tok_rows + local_index for offset in range(reach_slabs + 1)]
    )
    doc_begin = query_index - positions
    distance = query_index[:, None] - key_index[None, :]
    visible = (distance >= 0) & (distance < window) & (key_index[None, :] >= doc_begin[:, None])
    scores = contract(query_rot, key_all)
    capped = soft_cap * jnp.tanh(scores / soft_cap)
    exp_scores = jnp.where(visible, jnp.exp(capped), 0.0)
    row_total = jnp.sum(exp_scores, axis=1)
    attn_rows = (
        jnp.dot(exp_scores.astype(jnp.bfloat16), value_all, preferred_element_type=jnp.float32)
        / row_total[:, None]
    ).astype(jnp.bfloat16)
    row_delta = jnp.sum(out_grad.astype(jnp.float32) * attn_rows.astype(jnp.float32), axis=1)
    soft_probs = exp_scores / row_total[:, None]
    prob_grad = contract(out_grad, value_all)
    score_grad = soft_probs * (prob_grad - row_delta[:, None]) * (1.0 - (capped / soft_cap) ** 2)
    score_low = score_grad.astype(jnp.bfloat16)
    probs_low = soft_probs.astype(jnp.bfloat16)
    rot_grad = jnp.dot(score_low, key_all, preferred_element_type=jnp.float32)
    query_grad = (rotate(rot_grad, cos_table, -sin_table) * query_scale).astype(jnp.bfloat16)
    key_grads = contract_rows(score_low, query_rot)
    value_grads = contract_rows(probs_low, out_grad)
    key_total = key_grads[:tok_rows]
    value_total = value_grads[:tok_rows]
    for offset in range(1, reach_slabs + 1):
        piece = jnp.concatenate(
            [
                key_grads[offset * tok_rows : (offset + 1) * tok_rows].astype(jnp.bfloat16),
                value_grads[offset * tok_rows : (offset + 1) * tok_rows].astype(jnp.bfloat16),
            ],
            axis=1,
        )
        recv = shifted(piece, "seq", -offset).astype(jnp.float32)
        key_total = key_total + recv[:, :HD]
        value_total = value_total + recv[:, HD:]
    outbound = jnp.where(is_even, value_total, key_total)
    partner_grad = from_partner(outbound.astype(jnp.bfloat16), "wt", 0).astype(outbound.dtype)
    pair_total = jnp.where(is_even, key_total, value_total) + partner_grad
    pair_grad = jnp.where(is_even, rotate(pair_total, cos_table, -sin_table), pair_total).astype(
        jnp.bfloat16
    )
    contribution = contract(w_query, query_grad) + contract(w_pair, pair_grad)
    row_part = jnp.sum(contribution * gained_full.T, axis=0)
    row_top = lax.reduce_precision(row_part, exponent_bits=8, mantissa_bits=7)
    row_hi = row_top.astype(jnp.bfloat16)
    row_lo = (row_part - row_top).astype(jnp.bfloat16)
    pad_rows = 16
    extra_rows = jnp.concatenate(
        [row_hi[None], row_lo[None], jnp.zeros((pad_rows - 2, tok_rows), jnp.bfloat16)], axis=0
    )
    packed = jnp.concatenate(
        [
            contribution.astype(jnp.bfloat16).reshape(groups, feat, tok_rows),
            jnp.broadcast_to(extra_rows[None], (groups, pad_rows, tok_rows)),
        ],
        axis=1,
    ).reshape(groups * (feat + pad_rows), tok_rows)
    scattered = jnp.sum(
        lax.all_to_all(
            packed.reshape(groups, feat + pad_rows, tok_rows),
            "wt",
            split_axis=0,
            concat_axis=0,
            tiled=True,
        ).astype(jnp.float32),
        axis=0,
    )
    normed_grad = scattered[:feat].astype(jnp.float32).T
    row_dots = scattered[feat].astype(jnp.float32) + scattered[feat + 1].astype(jnp.float32)
    scaled_grad = normed_grad * norm_gain[None, :]
    tokens_grad = (inv_rms[:, None] * (scaled_grad - scaled * (row_dots / D)[:, None])).astype(
        jnp.bfloat16
    )
    gain_part = jnp.sum(normed_grad * scaled, axis=0)
    grad_query = contract_rows(normed, query_grad)
    grad_pair = contract_rows(normed, pair_grad)
    grad_table = jnp.concatenate(
        [
            grad_query.reshape(row_blocks, BLK, BLK),
            grad_pair.reshape(row_blocks, BLK, BLK),
            jnp.zeros((1, BLK, BLK), jnp.float32),
        ],
        axis=0,
    )
    slot_grads = grad_table[arrival].reshape(groups, CAP, BLK, BLK)
    empty_block = jnp.zeros((1, BLK, BLK), jnp.bfloat16)
    returned = lax.all_to_all(
        slot_grads.astype(jnp.bfloat16), "wt", split_axis=0, concat_axis=0, tiled=True
    )
    owned_grads = jnp.concatenate([returned.reshape(-1, BLK, BLK), empty_block], axis=0)[slot_dest]
    n_seq = lax.axis_size("seq")
    slots = owned_grads.shape[0]
    chunk = slots * BLK * BLK // n_seq
    gain_width = -(-feat // 128) * 128
    gain_row = jnp.pad(gain_part.astype(jnp.bfloat16), (0, gain_width - feat))
    to_reduce = jnp.concatenate(
        [
            owned_grads.reshape(n_seq, chunk),
            jnp.broadcast_to(gain_row[None], (n_seq, gain_width)),
        ],
        axis=1,
    )
    reduced = jnp.sum(
        lax.all_to_all(to_reduce, "seq", split_axis=0, concat_axis=0, tiled=True).astype(
            jnp.float32
        ),
        axis=0,
    )
    block_grads = lax.all_gather(
        reduced[:chunk].astype(jnp.bfloat16).reshape(slots // n_seq, BLK, BLK),
        "seq",
        axis=0,
        tiled=True,
    )
    gain_total = reduced[chunk : chunk + feat]
    return (attn_rows, tokens_grad, gain_total, block_grads[None])


def solution(mesh):
    placed = (
        P("seq", "wt"),
        P("wt"),
        P("seq"),
        P("wt", None, None, None),
        P("wt", None),
        P("seq", "wt"),
    )
    return jax.shard_map(
        body,
        mesh=mesh,
        in_specs=placed,
        out_specs=(P("seq", "wt"), P("seq", "wt"), P("wt"), P("wt", None, None, None)),
        check_vma=False,
    )
```

```python
import jax
import jax.numpy as jnp
from jax import lax
from jax.sharding import PartitionSpec as P

D = 4608
HD = 128
BLK = 128
CAP = 2


query_scale = 144.0 ** (-0.5)
soft_cap = 50.0
norm_eps = 1e-06


def from_partner(block, axis, stride):
    count = lax.axis_size(axis)
    route = []
    for low in range(count):
        high = low | 1 << stride
        if high != low and high < count:
            route += [(low, high), (high, low)]
    return lax.ppermute(block, axis, route)


def shifted(value, axis, steps):
    count = lax.axis_size(axis)
    initial, last = (max(0, -steps), min(count, count - steps))
    return lax.ppermute(value, axis, [(source, source + steps) for source in range(initial, last)])


def rope_tables(positions, head_width):
    half_width = head_width // 2
    frequency = 10000.0 ** (-2.0 * jnp.arange(half_width, dtype=jnp.float32) / head_width)
    angles = positions.astype(jnp.float32)[:, None] * frequency[None, :]
    return (jnp.cos(angles), jnp.sin(angles))


def rotate(vector, cos_table, sin_table):
    half_width = vector.shape[-1] // 2
    first_half = vector[..., :half_width]
    second_half = vector[..., half_width:]
    return jnp.concatenate(
        [
            first_half * cos_table - second_half * sin_table,
            first_half * sin_table + second_half * cos_table,
        ],
        axis=-1,
    )


def contract(left, right):
    return lax.dot_general(
        left, right, (((1,), (1,)), ((), ())), preferred_element_type=jnp.float32
    )


def contract_rows(left, right):
    return lax.dot_general(
        left, right, (((0,), (0,)), ((), ())), preferred_element_type=jnp.float32
    )


def body(tokens_in, norm_gain, positions, blocks, slot_code, out_grad):
    tok_rows = tokens_in.shape[0]
    feat = tokens_in.shape[1]
    groups = lax.axis_size("wt")
    slab_index = lax.axis_index("seq")
    is_even = lax.axis_index("wt") % 2 == 0
    pos_count = 2 * (D // BLK)
    row_blocks = pos_count // 2
    slot_codes = slot_code[0]
    is_live = slot_codes >= 0
    target_user = jnp.where(is_live, slot_codes // pos_count, 0)
    user_match = (
        (target_user[:, None] == jnp.arange(groups, dtype=jnp.int32)[None, :]) & is_live[:, None]
    ).astype(jnp.int32)
    earlier = jnp.cumsum(user_match, axis=0) - user_match
    slot_rank = jnp.sum(earlier * user_match, axis=1)
    dump_slot = groups * CAP
    slot_dest = jnp.where(is_live, target_user * CAP + slot_rank, dump_slot)
    block_place = (slot_codes - target_user * pos_count).astype(jnp.float32)
    outgoing = jnp.zeros((dump_slot + 1, BLK, BLK), jnp.bfloat16).at[slot_dest].set(blocks[0])
    outgoing_pos = (
        jnp.full((dump_slot + 1,), -1.0, jnp.float32)
        .at[slot_dest]
        .set(block_place)
        .astype(jnp.bfloat16)
    )
    arrived, arrived_pos = (
        lax.all_to_all(
            outgoing[:dump_slot].reshape(groups, CAP, BLK, BLK),
            "wt",
            split_axis=0,
            concat_axis=0,
            tiled=True,
        ),
        lax.all_to_all(
            outgoing_pos[:dump_slot].reshape(groups, CAP),
            "wt",
            split_axis=0,
            concat_axis=0,
            tiled=True,
        ),
    )
    gain_hi = lax.reduce_precision(norm_gain, exponent_bits=8, mantissa_bits=7)
    gain_rest = norm_gain - gain_hi
    gain_mid = lax.reduce_precision(gain_rest, exponent_bits=8, mantissa_bits=7)
    gain_lo = gain_rest - gain_mid
    gain_rows = jnp.stack([gain_hi, gain_mid, gain_lo]).astype(jnp.bfloat16)
    side_rows = 8
    gathered = lax.all_gather(
        jnp.concatenate(
            [tokens_in, gain_rows, jnp.zeros((side_rows - 3, feat), jnp.bfloat16)], axis=0
        ),
        "wt",
        axis=1,
        tiled=True,
    )
    tokens_full = gathered[:tok_rows]
    gain_parts = gathered[tok_rows : tok_rows + 3].astype(jnp.float32)
    gain_full = (gain_parts[0] + gain_parts[1]) + gain_parts[2]
    full_f32 = tokens_full.astype(jnp.float32)
    squares = jnp.sum(full_f32 * full_f32, axis=1)
    inv_rms = lax.rsqrt(squares / D + norm_eps)
    scaled_full = full_f32 * inv_rms[:, None]
    gained_full = scaled_full * gain_full[None, :]
    normed = gained_full.astype(jnp.bfloat16)
    scaled = tokens_in.astype(jnp.float32) * inv_rms[:, None]
    arrival = arrived_pos.reshape(-1).astype(jnp.int32)
    arrival = jnp.where(arrival < 0, pos_count, arrival)
    weight_table = (
        jnp.zeros((pos_count + 1, BLK, BLK), jnp.bfloat16)
        .at[arrival]
        .set(arrived.reshape(-1, BLK, BLK))
    )
    w_query = weight_table[:row_blocks].reshape(D, HD)
    w_pair = weight_table[row_blocks:pos_count].reshape(D, HD)
    query_proj = jnp.dot(normed, w_query, preferred_element_type=jnp.float32)
    pair_proj = jnp.dot(normed, w_pair, preferred_element_type=jnp.float32)
    cos_table, sin_table = rope_tables(positions, HD)
    query_rot = (rotate(query_proj, cos_table, sin_table) * query_scale).astype(jnp.bfloat16)
    own_pair = jnp.where(is_even, rotate(pair_proj, cos_table, sin_table), pair_proj).astype(
        jnp.bfloat16
    )
    partner = from_partner(own_pair, "wt", 0)
    key_rows = jnp.where(is_even, own_pair, partner)
    value_rows = jnp.where(is_even, partner, own_pair)
    reach_slabs = lax.axis_size("seq") // 2
    window = reach_slabs * tok_rows
    key_value = jnp.concatenate([key_rows, value_rows], axis=1)
    key_list = [key_rows]
    value_list = [value_rows]
    for offset in range(1, reach_slabs + 1):
        prev = shifted(key_value, "seq", offset)
        key_list.append(prev[:, :HD])
        value_list.append(prev[:, HD:])
    key_all = jnp.concatenate(key_list, axis=0)
    value_all = jnp.concatenate(value_list, axis=0)
    local_index = jnp.arange(tok_rows, dtype=jnp.int32)
    query_index = slab_index * tok_rows + local_index
    key_index = jnp.concatenate(
        [(slab_index - offset) * tok_rows + local_index for offset in range(reach_slabs + 1)]
    )
    doc_begin = query_index - positions
    distance = query_index[:, None] - key_index[None, :]
    visible = (distance >= 0) & (distance < window) & (key_index[None, :] >= doc_begin[:, None])
    scores = contract(query_rot, key_all)
    capped = soft_cap * jnp.tanh(scores / soft_cap)
    exp_scores = jnp.where(visible, jnp.exp(capped), 0.0)
    row_total = jnp.sum(exp_scores, axis=1)
    attn_rows = (
        jnp.dot(exp_scores.astype(jnp.bfloat16), value_all, preferred_element_type=jnp.float32)
        / row_total[:, None]
    ).astype(jnp.bfloat16)
    row_delta = jnp.sum(out_grad.astype(jnp.float32) * attn_rows.astype(jnp.float32), axis=1)
    soft_probs = exp_scores / row_total[:, None]
    prob_grad = contract(out_grad, value_all)
    score_grad = soft_probs * (prob_grad - row_delta[:, None]) * (1.0 - (capped / soft_cap) ** 2)
    score_low = score_grad.astype(jnp.bfloat16)
    probs_low = soft_probs.astype(jnp.bfloat16)
    rot_grad = jnp.dot(score_low, key_all, preferred_element_type=jnp.float32)
    query_grad = (rotate(rot_grad, cos_table, -sin_table) * query_scale).astype(jnp.bfloat16)
    key_grads = contract_rows(score_low, query_rot)
    value_grads = contract_rows(probs_low, out_grad)
    key_total = key_grads[:tok_rows]
    value_total = value_grads[:tok_rows]
    for offset in range(1, reach_slabs + 1):
        piece = jnp.concatenate(
            [
                key_grads[offset * tok_rows : (offset + 1) * tok_rows].astype(jnp.bfloat16),
                value_grads[offset * tok_rows : (offset + 1) * tok_rows].astype(jnp.bfloat16),
            ],
            axis=1,
        )
        recv = shifted(piece, "seq", -offset).astype(jnp.float32)
        key_total = key_total + recv[:, :HD]
        value_total = value_total + recv[:, HD:]
    outbound = jnp.where(is_even, value_total, key_total)
    partner_grad = from_partner(outbound.astype(jnp.bfloat16), "wt", 0).astype(outbound.dtype)
    pair_total = jnp.where(is_even, key_total, value_total) + partner_grad
    pair_grad = jnp.where(is_even, rotate(pair_total, cos_table, -sin_table), pair_total).astype(
        jnp.bfloat16
    )
    contribution = contract(w_query, query_grad) + contract(w_pair, pair_grad)
    row_part = jnp.sum(contribution * gained_full.T, axis=0)
    row_top = lax.reduce_precision(row_part, exponent_bits=8, mantissa_bits=7)
    row_hi = row_top.astype(jnp.bfloat16)
    row_lo = (row_part - row_top).astype(jnp.bfloat16)
    pad_rows = 16
    extra_rows = jnp.concatenate(
        [row_hi[None], row_lo[None], jnp.zeros((pad_rows - 2, tok_rows), jnp.bfloat16)], axis=0
    )
    packed = jnp.concatenate(
        [
            contribution.astype(jnp.bfloat16).reshape(groups, feat, tok_rows),
            jnp.broadcast_to(extra_rows[None], (groups, pad_rows, tok_rows)),
        ],
        axis=1,
    ).reshape(groups * (feat + pad_rows), tok_rows)
    scattered = jnp.sum(
        lax.all_to_all(
            packed.reshape(groups, feat + pad_rows, tok_rows),
            "wt",
            split_axis=0,
            concat_axis=0,
            tiled=True,
        ).astype(jnp.float32),
        axis=0,
    )
    normed_grad = scattered[:feat].astype(jnp.float32).T
    row_dots = scattered[feat].astype(jnp.float32) + scattered[feat + 1].astype(jnp.float32)
    scaled_grad = normed_grad * norm_gain[None, :]
    tokens_grad = (inv_rms[:, None] * (scaled_grad - scaled * (row_dots / D)[:, None])).astype(
        jnp.bfloat16
    )
    gain_part = jnp.sum(normed_grad * scaled, axis=0)
    grad_query = contract_rows(normed, query_grad)
    grad_pair = contract_rows(normed, pair_grad)
    grad_table = jnp.concatenate(
        [
            grad_query.reshape(row_blocks, BLK, BLK),
            grad_pair.reshape(row_blocks, BLK, BLK),
            jnp.zeros((1, BLK, BLK), jnp.float32),
        ],
        axis=0,
    )
    slot_grads = grad_table[arrival].reshape(groups, CAP, BLK, BLK)
    empty_block = jnp.zeros((1, BLK, BLK), jnp.bfloat16)
    returned = lax.all_to_all(
        slot_grads.astype(jnp.bfloat16), "wt", split_axis=0, concat_axis=0, tiled=True
    )
    owned_grads = jnp.concatenate([returned.reshape(-1, BLK, BLK), empty_block], axis=0)[slot_dest]
    n_seq = lax.axis_size("seq")
    slots = owned_grads.shape[0]
    chunk = slots * BLK * BLK // n_seq
    gain_width = -(-feat // 128) * 128
    reduced = lax.psum_scatter(owned_grads, "seq", scatter_dimension=0, tiled=True)
    gain_row = jnp.pad(gain_part.astype(jnp.bfloat16), (0, gain_width - feat))
    gathered_back = lax.all_gather(
        jnp.concatenate([reduced.reshape(1, chunk), gain_row[None]], axis=1),
        "seq",
        axis=0,
        tiled=True,
    )
    block_grads = gathered_back[:, :chunk].reshape(slots, BLK, BLK)
    gain_total = jnp.sum(gathered_back[:, chunk : chunk + feat].astype(jnp.float32), axis=0)
    return (attn_rows, tokens_grad, gain_total, block_grads[None])


def solution(mesh):
    placed = (
        P("seq", "wt"),
        P("wt"),
        P("seq"),
        P("wt", None, None, None),
        P("wt", None),
        P("seq", "wt"),
    )
    return jax.shard_map(
        body,
        mesh=mesh,
        in_specs=placed,
        out_specs=(P("seq", "wt"), P("seq", "wt"), P("wt"), P("wt", None, None, None)),
        check_vma=False,
    )
```

```python
import jax
import jax.numpy as jnp
from jax import lax
from jax.sharding import PartitionSpec as P

D = 4608
HD = 128
BLK = 128
CAP = 2


query_scale = 144.0 ** (-0.5)
soft_cap = 50.0
norm_eps = 1e-06


def from_partner(block, axis, stride):
    count = lax.axis_size(axis)
    route = []
    for low in range(count):
        high = low | 1 << stride
        if high != low and high < count:
            route += [(low, high), (high, low)]
    return lax.ppermute(block, axis, route)


def shifted(value, axis, steps):
    count = lax.axis_size(axis)
    initial, last = (max(0, -steps), min(count, count - steps))
    return lax.ppermute(value, axis, [(source, source + steps) for source in range(initial, last)])


def rope_tables(positions, head_width):
    half_width = head_width // 2
    frequency = 10000.0 ** (-2.0 * jnp.arange(half_width, dtype=jnp.float32) / head_width)
    angles = positions.astype(jnp.float32)[:, None] * frequency[None, :]
    return (jnp.cos(angles), jnp.sin(angles))


def rotate(vector, cos_table, sin_table):
    half_width = vector.shape[-1] // 2
    first_half = vector[..., :half_width]
    second_half = vector[..., half_width:]
    return jnp.concatenate(
        [
            first_half * cos_table - second_half * sin_table,
            first_half * sin_table + second_half * cos_table,
        ],
        axis=-1,
    )


def contract(left, right):
    return lax.dot_general(
        left, right, (((1,), (1,)), ((), ())), preferred_element_type=jnp.float32
    )


def contract_rows(left, right):
    return lax.dot_general(
        left, right, (((0,), (0,)), ((), ())), preferred_element_type=jnp.float32
    )


def body(tokens_in, norm_gain, positions, blocks, slot_code, out_grad):
    tok_rows = tokens_in.shape[0]
    feat = tokens_in.shape[1]
    groups = lax.axis_size("wt")
    slab_index = lax.axis_index("seq")
    is_even = lax.axis_index("wt") % 2 == 0
    pos_count = 2 * (D // BLK)
    row_blocks = pos_count // 2
    slot_codes = slot_code[0]
    is_live = slot_codes >= 0
    target_user = jnp.where(is_live, slot_codes // pos_count, 0)
    user_match = (
        (target_user[:, None] == jnp.arange(groups, dtype=jnp.int32)[None, :]) & is_live[:, None]
    ).astype(jnp.int32)
    earlier = jnp.cumsum(user_match, axis=0) - user_match
    slot_rank = jnp.sum(earlier * user_match, axis=1)
    dump_slot = groups * CAP
    slot_dest = jnp.where(is_live, target_user * CAP + slot_rank, dump_slot)
    block_place = (slot_codes - target_user * pos_count).astype(jnp.float32)
    outgoing = jnp.zeros((dump_slot + 1, BLK, BLK), jnp.bfloat16).at[slot_dest].set(blocks[0])
    outgoing_pos = (
        jnp.full((dump_slot + 1,), -1.0, jnp.float32)
        .at[slot_dest]
        .set(block_place)
        .astype(jnp.bfloat16)
    )
    arrived, arrived_pos = (
        lax.all_to_all(
            outgoing[:dump_slot].reshape(groups, CAP, BLK, BLK),
            "wt",
            split_axis=0,
            concat_axis=0,
            tiled=True,
        ),
        lax.all_to_all(
            outgoing_pos[:dump_slot].reshape(groups, CAP),
            "wt",
            split_axis=0,
            concat_axis=0,
            tiled=True,
        ),
    )
    gain_hi = lax.reduce_precision(norm_gain, exponent_bits=8, mantissa_bits=7)
    gain_rest = norm_gain - gain_hi
    gain_mid = lax.reduce_precision(gain_rest, exponent_bits=8, mantissa_bits=7)
    gain_lo = gain_rest - gain_mid
    gain_rows = jnp.stack([gain_hi, gain_mid, gain_lo]).astype(jnp.bfloat16)
    side_rows = 8
    gathered = lax.all_gather(
        jnp.concatenate(
            [tokens_in, gain_rows, jnp.zeros((side_rows - 3, feat), jnp.bfloat16)], axis=0
        ),
        "wt",
        axis=1,
        tiled=True,
    )
    tokens_full = gathered[:tok_rows]
    gain_parts = gathered[tok_rows : tok_rows + 3].astype(jnp.float32)
    gain_full = (gain_parts[0] + gain_parts[1]) + gain_parts[2]
    full_f32 = tokens_full.astype(jnp.float32)
    squares = jnp.sum(full_f32 * full_f32, axis=1)
    inv_rms = lax.rsqrt(squares / D + norm_eps)
    scaled_full = full_f32 * inv_rms[:, None]
    gained_full = scaled_full * gain_full[None, :]
    normed = gained_full.astype(jnp.bfloat16)
    scaled = tokens_in.astype(jnp.float32) * inv_rms[:, None]
    arrival = arrived_pos.reshape(-1).astype(jnp.int32)
    arrival = jnp.where(arrival < 0, pos_count, arrival)
    weight_table = (
        jnp.zeros((pos_count + 1, BLK, BLK), jnp.bfloat16)
        .at[arrival]
        .set(arrived.reshape(-1, BLK, BLK))
    )
    w_query = weight_table[:row_blocks].reshape(D, HD)
    w_pair = weight_table[row_blocks:pos_count].reshape(D, HD)
    query_proj = jnp.dot(normed, w_query, preferred_element_type=jnp.float32)
    pair_proj = jnp.dot(normed, w_pair, preferred_element_type=jnp.float32)
    cos_table, sin_table = rope_tables(positions, HD)
    query_rot = (rotate(query_proj, cos_table, sin_table) * query_scale).astype(jnp.bfloat16)
    own_pair = jnp.where(is_even, rotate(pair_proj, cos_table, sin_table), pair_proj).astype(
        jnp.bfloat16
    )
    partner = from_partner(own_pair, "wt", 0)
    key_rows = jnp.where(is_even, own_pair, partner)
    value_rows = jnp.where(is_even, partner, own_pair)
    reach_slabs = lax.axis_size("seq") // 2
    window = reach_slabs * tok_rows
    key_value = jnp.concatenate([key_rows, value_rows], axis=1)
    key_list = [key_rows]
    value_list = [value_rows]
    for offset in range(1, reach_slabs + 1):
        prev = shifted(key_value, "seq", offset)
        key_list.append(prev[:, :HD])
        value_list.append(prev[:, HD:])
    key_all = jnp.concatenate(key_list, axis=0)
    value_all = jnp.concatenate(value_list, axis=0)
    local_index = jnp.arange(tok_rows, dtype=jnp.int32)
    query_index = slab_index * tok_rows + local_index
    key_index = jnp.concatenate(
        [(slab_index - offset) * tok_rows + local_index for offset in range(reach_slabs + 1)]
    )
    doc_begin = query_index - positions
    distance = query_index[:, None] - key_index[None, :]
    visible = (distance >= 0) & (distance < window) & (key_index[None, :] >= doc_begin[:, None])
    scores = contract(query_rot, key_all)
    capped = soft_cap * jnp.tanh(scores / soft_cap)
    exp_scores = jnp.where(visible, jnp.exp(capped), 0.0)
    row_total = jnp.sum(exp_scores, axis=1)
    attn_rows = (
        jnp.dot(exp_scores.astype(jnp.bfloat16), value_all, preferred_element_type=jnp.float32)
        / row_total[:, None]
    ).astype(jnp.bfloat16)
    row_delta = jnp.sum(out_grad.astype(jnp.float32) * attn_rows.astype(jnp.float32), axis=1)
    soft_probs = exp_scores / row_total[:, None]
    prob_grad = contract(out_grad, value_all)
    score_grad = soft_probs * (prob_grad - row_delta[:, None]) * (1.0 - (capped / soft_cap) ** 2)
    score_low = score_grad.astype(jnp.bfloat16)
    probs_low = soft_probs.astype(jnp.bfloat16)
    rot_grad = jnp.dot(score_low, key_all, preferred_element_type=jnp.float32)
    query_grad = (rotate(rot_grad, cos_table, -sin_table) * query_scale).astype(jnp.bfloat16)
    key_grads = contract_rows(score_low, query_rot)
    value_grads = contract_rows(probs_low, out_grad)
    key_total = key_grads[:tok_rows]
    value_total = value_grads[:tok_rows]
    for offset in range(1, reach_slabs + 1):
        piece = jnp.concatenate(
            [
                key_grads[offset * tok_rows : (offset + 1) * tok_rows].astype(jnp.bfloat16),
                value_grads[offset * tok_rows : (offset + 1) * tok_rows].astype(jnp.bfloat16),
            ],
            axis=1,
        )
        recv = shifted(piece, "seq", -offset).astype(jnp.float32)
        key_total = key_total + recv[:, :HD]
        value_total = value_total + recv[:, HD:]
    outbound = jnp.where(is_even, value_total, key_total)
    partner_grad = from_partner(outbound.astype(jnp.bfloat16), "wt", 0).astype(outbound.dtype)
    pair_total = jnp.where(is_even, key_total, value_total) + partner_grad
    pair_grad = jnp.where(is_even, rotate(pair_total, cos_table, -sin_table), pair_total).astype(
        jnp.bfloat16
    )
    contribution = contract(w_query, query_grad) + contract(w_pair, pair_grad)
    row_part = jnp.sum(contribution * gained_full.T, axis=0)
    row_top = lax.reduce_precision(row_part, exponent_bits=8, mantissa_bits=7)
    row_hi = row_top.astype(jnp.bfloat16)
    row_lo = (row_part - row_top).astype(jnp.bfloat16)
    pad_rows = 16
    extra_rows = jnp.concatenate(
        [row_hi[None], row_lo[None], jnp.zeros((pad_rows - 2, tok_rows), jnp.bfloat16)], axis=0
    )
    packed = jnp.concatenate(
        [
            contribution.astype(jnp.bfloat16).reshape(groups, feat, tok_rows),
            jnp.broadcast_to(extra_rows[None], (groups, pad_rows, tok_rows)),
        ],
        axis=1,
    ).reshape(groups * (feat + pad_rows), tok_rows)
    scattered = jnp.sum(
        lax.all_to_all(
            packed.reshape(groups, feat + pad_rows, tok_rows),
            "wt",
            split_axis=0,
            concat_axis=0,
            tiled=True,
        ).astype(jnp.float32),
        axis=0,
    )
    normed_grad = scattered[:feat].astype(jnp.float32).T
    row_dots = scattered[feat].astype(jnp.float32) + scattered[feat + 1].astype(jnp.float32)
    scaled_grad = normed_grad * norm_gain[None, :]
    tokens_grad = (inv_rms[:, None] * (scaled_grad - scaled * (row_dots / D)[:, None])).astype(
        jnp.bfloat16
    )
    grad_query = contract_rows(normed, query_grad)
    grad_pair = contract_rows(normed, pair_grad)
    grad_table = jnp.concatenate(
        [
            grad_query.reshape(row_blocks, BLK, BLK),
            grad_pair.reshape(row_blocks, BLK, BLK),
            jnp.zeros((1, BLK, BLK), jnp.float32),
        ],
        axis=0,
    )
    n_seq = lax.axis_size("seq")
    band = BLK // n_seq
    slots = slot_dest.shape[0]
    band_len = CAP * band * BLK
    block_len = groups * band_len
    slot_grads = grad_table[arrival].astype(jnp.bfloat16).reshape(groups, CAP, n_seq, band, BLK)
    block_send = jnp.transpose(slot_grads, (2, 0, 1, 3, 4)).reshape(n_seq, block_len)
    gain_width = D // n_seq
    per_chunk = gain_width // feat
    head_gain = jnp.sum(contribution * scaled_full.T, axis=1)
    head_top = lax.reduce_precision(head_gain, exponent_bits=8, mantissa_bits=7)
    head_pair = jnp.stack([head_top, head_gain - head_top]).astype(jnp.bfloat16)
    gain_send = jnp.transpose(head_pair.reshape(2, n_seq, gain_width), (1, 0, 2)).reshape(
        n_seq, 2 * gain_width
    )
    gain_pad = -(-(2 * gain_width) // 128) * 128 - 2 * gain_width
    seq_recv = lax.all_to_all(
        jnp.concatenate(
            [block_send, gain_send, jnp.zeros((n_seq, gain_pad), jnp.bfloat16)], axis=1
        ),
        "seq",
        split_axis=0,
        concat_axis=0,
        tiled=True,
    )
    seq_sum = jnp.sum(seq_recv.astype(jnp.float32), axis=0)
    block_chunk = seq_sum[:block_len].astype(jnp.bfloat16).reshape(groups, band_len)
    gain_chunk = (
        seq_sum[block_len : block_len + gain_width]
        + seq_sum[block_len + gain_width : block_len + 2 * gain_width]
    )
    chunk_top = lax.reduce_precision(gain_chunk, exponent_bits=8, mantissa_bits=7)
    chunk_pair = jnp.stack([chunk_top, gain_chunk - chunk_top]).astype(jnp.bfloat16)
    chunk_dest = jnp.transpose(chunk_pair.reshape(2, per_chunk, feat), (1, 0, 2)).reshape(
        per_chunk, 2 * feat
    )
    gain_slots = lax.dynamic_update_slice(
        jnp.zeros((groups, 2 * feat), jnp.bfloat16), chunk_dest, (slab_index * per_chunk, 0)
    )
    slot_pad = -(-(2 * feat) // 128) * 128 - 2 * feat
    wt_recv = lax.all_to_all(
        jnp.concatenate(
            [block_chunk, gain_slots, jnp.zeros((groups, slot_pad), jnp.bfloat16)], axis=1
        ),
        "wt",
        split_axis=0,
        concat_axis=0,
        tiled=True,
    )
    returned = wt_recv[:, :band_len].reshape(groups * CAP, band, BLK)
    owned_band = jnp.concatenate([returned, jnp.zeros((1, band, BLK), jnp.bfloat16)], axis=0)[
        slot_dest
    ]
    gain_recv = wt_recv[:, band_len : band_len + 2 * feat].astype(jnp.float32)
    gain_mine = jnp.sum(gain_recv[:, :feat] + gain_recv[:, feat:], axis=0)
    mine_top = lax.reduce_precision(gain_mine, exponent_bits=8, mantissa_bits=7)
    mine_pair = jnp.stack([mine_top, gain_mine - mine_top]).astype(jnp.bfloat16).reshape(-1)
    owned_len = slots * band * BLK
    send_len = -(-(owned_len + 2 * feat) // 1024) * 1024
    gather_send = jnp.concatenate(
        [
            owned_band.reshape(-1),
            mine_pair,
            jnp.zeros((send_len - owned_len - 2 * feat,), jnp.bfloat16),
        ]
    ).reshape(send_len // 128, 128)
    gathered_back = lax.all_gather(gather_send, "seq", axis=0, tiled=True).reshape(
        n_seq, send_len
    )
    block_grads = jnp.transpose(
        gathered_back[:, :owned_len].reshape(n_seq, slots, band, BLK), (1, 0, 2, 3)
    ).reshape(slots, BLK, BLK)
    gain_total = jnp.sum(
        gathered_back[:, owned_len : owned_len + feat].astype(jnp.float32)
        + gathered_back[:, owned_len + feat : owned_len + 2 * feat].astype(jnp.float32),
        axis=0,
    )
    return (attn_rows, tokens_grad, gain_total, block_grads[None])


def solution(mesh):
    placed = (
        P("seq", "wt"),
        P("wt"),
        P("seq"),
        P("wt", None, None, None),
        P("wt", None),
        P("seq", "wt"),
    )
    return jax.shard_map(
        body,
        mesh=mesh,
        in_specs=placed,
        out_specs=(P("seq", "wt"), P("seq", "wt"), P("wt"), P("wt", None, None, None)),
        check_vma=False,
    )
```

```python
import jax
import jax.numpy as jnp
from jax import lax
from jax.sharding import PartitionSpec as P

D = 4608
HD = 128
BLK = 128
CAP = 2


query_scale = 144.0 ** (-0.5)
soft_cap = 50.0
norm_eps = 1e-06


def from_partner(block, axis, stride):
    count = lax.axis_size(axis)
    route = []
    for low in range(count):
        high = low | 1 << stride
        if high != low and high < count:
            route += [(low, high), (high, low)]
    return lax.ppermute(block, axis, route)


def shifted(value, axis, steps):
    count = lax.axis_size(axis)
    initial, last = (max(0, -steps), min(count, count - steps))
    return lax.ppermute(value, axis, [(source, source + steps) for source in range(initial, last)])


def rope_tables(positions, head_width):
    half_width = head_width // 2
    frequency = 10000.0 ** (-2.0 * jnp.arange(half_width, dtype=jnp.float32) / head_width)
    angles = positions.astype(jnp.float32)[:, None] * frequency[None, :]
    return (jnp.cos(angles), jnp.sin(angles))


def rotate(vector, cos_table, sin_table):
    half_width = vector.shape[-1] // 2
    first_half = vector[..., :half_width]
    second_half = vector[..., half_width:]
    return jnp.concatenate(
        [
            first_half * cos_table - second_half * sin_table,
            first_half * sin_table + second_half * cos_table,
        ],
        axis=-1,
    )


def contract(left, right):
    return lax.dot_general(
        left, right, (((1,), (1,)), ((), ())), preferred_element_type=jnp.float32
    )


def contract_rows(left, right):
    return lax.dot_general(
        left, right, (((0,), (0,)), ((), ())), preferred_element_type=jnp.float32
    )


def body(tokens_in, norm_gain, positions, blocks, slot_code, out_grad):
    tok_rows = tokens_in.shape[0]
    feat = tokens_in.shape[1]
    groups = lax.axis_size("wt")
    slab_index = lax.axis_index("seq")
    is_even = lax.axis_index("wt") % 2 == 0
    pos_count = 2 * (D // BLK)
    row_blocks = pos_count // 2
    slot_codes = slot_code[0]
    is_live = slot_codes >= 0
    target_user = jnp.where(is_live, slot_codes // pos_count, 0)
    user_match = (
        (target_user[:, None] == jnp.arange(groups, dtype=jnp.int32)[None, :]) & is_live[:, None]
    ).astype(jnp.int32)
    earlier = jnp.cumsum(user_match, axis=0) - user_match
    slot_rank = jnp.sum(earlier * user_match, axis=1)
    dump_slot = groups * CAP
    slot_dest = jnp.where(is_live, target_user * CAP + slot_rank, dump_slot)
    block_place = (slot_codes - target_user * pos_count).astype(jnp.float32)
    outgoing = jnp.zeros((dump_slot + 1, BLK, BLK), jnp.bfloat16).at[slot_dest].set(blocks[0])
    outgoing_pos = (
        jnp.full((dump_slot + 1,), -1.0, jnp.float32)
        .at[slot_dest]
        .set(block_place)
        .astype(jnp.bfloat16)
    )
    arrived, arrived_pos = (
        lax.all_to_all(
            outgoing[:dump_slot].reshape(groups, CAP, BLK, BLK),
            "wt",
            split_axis=0,
            concat_axis=0,
            tiled=True,
        ),
        lax.all_to_all(
            outgoing_pos[:dump_slot].reshape(groups, CAP),
            "wt",
            split_axis=0,
            concat_axis=0,
            tiled=True,
        ),
    )
    gain_hi = lax.reduce_precision(norm_gain, exponent_bits=8, mantissa_bits=7)
    gain_rest = norm_gain - gain_hi
    gain_mid = lax.reduce_precision(gain_rest, exponent_bits=8, mantissa_bits=7)
    gain_lo = gain_rest - gain_mid
    gain_rows = jnp.stack([gain_hi, gain_mid, gain_lo]).astype(jnp.bfloat16)
    side_rows = 8
    gathered = lax.all_gather(
        jnp.concatenate(
            [tokens_in, gain_rows, jnp.zeros((side_rows - 3, feat), jnp.bfloat16)], axis=0
        ),
        "wt",
        axis=1,
        tiled=True,
    )
    tokens_full = gathered[:tok_rows]
    gain_parts = gathered[tok_rows : tok_rows + 3].astype(jnp.float32)
    gain_full = (gain_parts[0] + gain_parts[1]) + gain_parts[2]
    full_f32 = tokens_full.astype(jnp.float32)
    squares = jnp.sum(full_f32 * full_f32, axis=1)
    inv_rms = lax.rsqrt(squares / D + norm_eps)
    scaled_full = full_f32 * inv_rms[:, None]
    gained_full = scaled_full * gain_full[None, :]
    normed = gained_full.astype(jnp.bfloat16)
    scaled = tokens_in.astype(jnp.float32) * inv_rms[:, None]
    arrival = arrived_pos.reshape(-1).astype(jnp.int32)
    arrival = jnp.where(arrival < 0, pos_count, arrival)
    weight_table = (
        jnp.zeros((pos_count + 1, BLK, BLK), jnp.bfloat16)
        .at[arrival]
        .set(arrived.reshape(-1, BLK, BLK))
    )
    w_query = weight_table[:row_blocks].reshape(D, HD)
    w_pair = weight_table[row_blocks:pos_count].reshape(D, HD)
    query_proj = jnp.dot(normed, w_query, preferred_element_type=jnp.float32)
    pair_proj = jnp.dot(normed, w_pair, preferred_element_type=jnp.float32)
    cos_table, sin_table = rope_tables(positions, HD)
    query_rot = (rotate(query_proj, cos_table, sin_table) * query_scale).astype(jnp.bfloat16)
    own_pair = jnp.where(is_even, rotate(pair_proj, cos_table, sin_table), pair_proj).astype(
        jnp.bfloat16
    )
    partner = from_partner(own_pair, "wt", 0)
    key_rows = jnp.where(is_even, own_pair, partner)
    value_rows = jnp.where(is_even, partner, own_pair)
    reach_slabs = lax.axis_size("seq") // 2
    window = reach_slabs * tok_rows
    key_value = jnp.concatenate([key_rows, value_rows], axis=1)
    key_list = [key_rows]
    value_list = [value_rows]
    for offset in range(1, reach_slabs + 1):
        prev = shifted(key_value, "seq", offset)
        key_list.append(prev[:, :HD])
        value_list.append(prev[:, HD:])
    key_all = jnp.concatenate(key_list, axis=0)
    value_all = jnp.concatenate(value_list, axis=0)
    local_index = jnp.arange(tok_rows, dtype=jnp.int32)
    query_index = slab_index * tok_rows + local_index
    key_index = jnp.concatenate(
        [(slab_index - offset) * tok_rows + local_index for offset in range(reach_slabs + 1)]
    )
    doc_begin = query_index - positions
    distance = query_index[:, None] - key_index[None, :]
    visible = (distance >= 0) & (distance < window) & (key_index[None, :] >= doc_begin[:, None])
    scores = contract(query_rot, key_all)
    capped = soft_cap * jnp.tanh(scores / soft_cap)
    exp_scores = jnp.where(visible, jnp.exp(capped), 0.0)
    row_total = jnp.sum(exp_scores, axis=1)
    attn_rows = (
        jnp.dot(exp_scores.astype(jnp.bfloat16), value_all, preferred_element_type=jnp.float32)
        / row_total[:, None]
    ).astype(jnp.bfloat16)
    row_delta = jnp.sum(out_grad.astype(jnp.float32) * attn_rows.astype(jnp.float32), axis=1)
    soft_probs = exp_scores / row_total[:, None]
    prob_grad = contract(out_grad, value_all)
    score_grad = soft_probs * (prob_grad - row_delta[:, None]) * (1.0 - (capped / soft_cap) ** 2)
    score_low = score_grad.astype(jnp.bfloat16)
    probs_low = soft_probs.astype(jnp.bfloat16)
    rot_grad = jnp.dot(score_low, key_all, preferred_element_type=jnp.float32)
    query_grad = (rotate(rot_grad, cos_table, -sin_table) * query_scale).astype(jnp.bfloat16)
    key_grads = contract_rows(score_low, query_rot)
    value_grads = contract_rows(probs_low, out_grad)
    key_total = key_grads[:tok_rows]
    value_total = value_grads[:tok_rows]
    for offset in range(1, reach_slabs + 1):
        piece = jnp.concatenate(
            [
                key_grads[offset * tok_rows : (offset + 1) * tok_rows].astype(jnp.bfloat16),
                value_grads[offset * tok_rows : (offset + 1) * tok_rows].astype(jnp.bfloat16),
            ],
            axis=1,
        )
        recv = shifted(piece, "seq", -offset).astype(jnp.float32)
        key_total = key_total + recv[:, :HD]
        value_total = value_total + recv[:, HD:]
    outbound = jnp.where(is_even, value_total, key_total)
    partner_grad = from_partner(outbound.astype(jnp.bfloat16), "wt", 0).astype(outbound.dtype)
    pair_total = jnp.where(is_even, key_total, value_total) + partner_grad
    pair_grad = jnp.where(is_even, rotate(pair_total, cos_table, -sin_table), pair_total).astype(
        jnp.bfloat16
    )
    contribution = contract(w_query, query_grad) + contract(w_pair, pair_grad)
    row_part = jnp.sum(contribution * gained_full.T, axis=0)
    row_top = lax.reduce_precision(row_part, exponent_bits=8, mantissa_bits=7)
    row_hi = row_top.astype(jnp.bfloat16)
    row_lo = (row_part - row_top).astype(jnp.bfloat16)
    pad_rows = 16
    extra_rows = jnp.concatenate(
        [row_hi[None], row_lo[None], jnp.zeros((pad_rows - 2, tok_rows), jnp.bfloat16)], axis=0
    )
    packed = jnp.concatenate(
        [
            contribution.astype(jnp.bfloat16).reshape(groups, feat, tok_rows),
            jnp.broadcast_to(extra_rows[None], (groups, pad_rows, tok_rows)),
        ],
        axis=1,
    ).reshape(groups * (feat + pad_rows), tok_rows)
    scattered = jnp.sum(
        lax.all_to_all(
            packed.reshape(groups, feat + pad_rows, tok_rows),
            "wt",
            split_axis=0,
            concat_axis=0,
            tiled=True,
        ).astype(jnp.float32),
        axis=0,
    )
    normed_grad = scattered[:feat].astype(jnp.float32).T
    row_dots = scattered[feat].astype(jnp.float32) + scattered[feat + 1].astype(jnp.float32)
    scaled_grad = normed_grad * norm_gain[None, :]
    tokens_grad = (inv_rms[:, None] * (scaled_grad - scaled * (row_dots / D)[:, None])).astype(
        jnp.bfloat16
    )
    grad_query = contract_rows(normed, query_grad)
    grad_pair = contract_rows(normed, pair_grad)
    grad_table = jnp.concatenate(
        [
            grad_query.reshape(row_blocks, BLK, BLK),
            grad_pair.reshape(row_blocks, BLK, BLK),
            jnp.zeros((1, BLK, BLK), jnp.float32),
        ],
        axis=0,
    )
    n_seq = lax.axis_size("seq")
    band = BLK // n_seq
    slots = slot_dest.shape[0]
    band_rows = CAP * band
    block_rows = groups * band_rows
    side = 16
    block_send = jnp.transpose(
        grad_table[arrival].reshape(groups, CAP, n_seq, band, BLK), (2, 0, 1, 3, 4)
    ).reshape(n_seq, block_rows, BLK)
    gain_width = D // n_seq
    per_chunk = gain_width // feat
    head_gain = jnp.sum(contribution * scaled_full.T, axis=1)
    head_top = lax.reduce_precision(head_gain, exponent_bits=8, mantissa_bits=7)
    head_pair = jnp.stack([head_top, head_gain - head_top]).astype(jnp.bfloat16)
    gain_send = jnp.transpose(head_pair.reshape(2, n_seq, gain_width), (1, 0, 2)).reshape(
        n_seq, 2 * gain_width
    )
    gain_send = jnp.pad(gain_send, ((0, 0), (0, side * BLK - 2 * gain_width))).reshape(
        n_seq, side, BLK
    )
    seq_recv = lax.all_to_all(
        jnp.concatenate([block_send.astype(jnp.bfloat16), gain_send], axis=1),
        "seq",
        split_axis=0,
        concat_axis=0,
        tiled=True,
    )
    seq_sum = jnp.sum(seq_recv.astype(jnp.float32), axis=0)
    block_chunk = seq_sum[:block_rows].astype(jnp.bfloat16).reshape(groups, band_rows, BLK)
    gain_flat = seq_sum[block_rows:].reshape(-1)
    gain_chunk = gain_flat[:gain_width] + gain_flat[gain_width : 2 * gain_width]
    chunk_top = lax.reduce_precision(gain_chunk, exponent_bits=8, mantissa_bits=7)
    chunk_pair = jnp.stack([chunk_top, gain_chunk - chunk_top]).astype(jnp.bfloat16)
    chunk_dest = jnp.transpose(chunk_pair.reshape(2, per_chunk, feat), (1, 0, 2)).reshape(
        per_chunk, 2 * feat
    )
    gain_slots = lax.dynamic_update_slice(
        jnp.zeros((groups, side * BLK), jnp.bfloat16), chunk_dest, (slab_index * per_chunk, 0)
    ).reshape(groups, side, BLK)
    wt_recv = lax.all_to_all(
        jnp.concatenate([block_chunk, gain_slots], axis=1),
        "wt",
        split_axis=0,
        concat_axis=0,
        tiled=True,
    )
    returned = wt_recv[:, :band_rows].astype(jnp.float32).reshape(groups * CAP, band, BLK)
    owned_band = jnp.concatenate([returned, jnp.zeros((1, band, BLK), jnp.float32)], axis=0)[
        slot_dest
    ]
    gain_recv = wt_recv[:, band_rows:].reshape(groups, side * BLK)[:, : 2 * feat]
    gain_recv = gain_recv.astype(jnp.float32)
    gain_mine = jnp.sum(gain_recv[:, :feat] + gain_recv[:, feat:], axis=0)
    mine_top = lax.reduce_precision(gain_mine, exponent_bits=8, mantissa_bits=7)
    mine_pair = jnp.stack([mine_top, gain_mine - mine_top]).astype(jnp.bfloat16).reshape(-1)
    owned_rows = slots * band
    gather_send = jnp.concatenate(
        [
            owned_band.reshape(owned_rows, BLK).astype(jnp.bfloat16),
            jnp.pad(mine_pair, (0, side * BLK - 2 * feat)).reshape(side, BLK),
        ],
        axis=0,
    )
    gathered_back = lax.all_gather(gather_send, "seq", axis=0, tiled=True).reshape(
        n_seq, owned_rows + side, BLK
    )
    block_grads = (
        jnp.transpose(
            gathered_back[:, :owned_rows]
            .astype(jnp.float32)
            .reshape(n_seq, slots, band, BLK),
            (1, 0, 2, 3),
        )
        .reshape(slots, BLK, BLK)
        .astype(jnp.bfloat16)
    )
    gain_back = gathered_back[:, owned_rows:].reshape(n_seq, side * BLK).astype(jnp.float32)
    gain_total = jnp.sum(gain_back[:, :feat] + gain_back[:, feat : 2 * feat], axis=0)
    return (attn_rows, tokens_grad, gain_total, block_grads[None])


def solution(mesh):
    placed = (
        P("seq", "wt"),
        P("wt"),
        P("seq"),
        P("wt", None, None, None),
        P("wt", None),
        P("seq", "wt"),
    )
    return jax.shard_map(
        body,
        mesh=mesh,
        in_specs=placed,
        out_specs=(P("seq", "wt"), P("seq", "wt"), P("wt"), P("wt", None, None, None)),
        check_vma=False,
    )
```

```python
import jax
import jax.numpy as jnp
from jax import lax
from jax.sharding import PartitionSpec as P

D = 4608
HD = 128
BLK = 128
CAP = 2


query_scale = 144.0 ** (-0.5)
soft_cap = 50.0
norm_eps = 1e-06


def from_partner(block, axis, stride):
    count = lax.axis_size(axis)
    route = []
    for low in range(count):
        high = low | 1 << stride
        if high != low and high < count:
            route += [(low, high), (high, low)]
    return lax.ppermute(block, axis, route)


def shifted(value, axis, steps):
    count = lax.axis_size(axis)
    initial, last = (max(0, -steps), min(count, count - steps))
    return lax.ppermute(value, axis, [(source, source + steps) for source in range(initial, last)])


def rope_tables(positions, head_width):
    half_width = head_width // 2
    frequency = 10000.0 ** (-2.0 * jnp.arange(half_width, dtype=jnp.float32) / head_width)
    angles = positions.astype(jnp.float32)[:, None] * frequency[None, :]
    return (jnp.cos(angles), jnp.sin(angles))


def rotate(vector, cos_table, sin_table):
    half_width = vector.shape[-1] // 2
    first_half = vector[..., :half_width]
    second_half = vector[..., half_width:]
    return jnp.concatenate(
        [
            first_half * cos_table - second_half * sin_table,
            first_half * sin_table + second_half * cos_table,
        ],
        axis=-1,
    )


def contract(left, right):
    return lax.dot_general(
        left, right, (((1,), (1,)), ((), ())), preferred_element_type=jnp.float32
    )


def contract_rows(left, right):
    return lax.dot_general(
        left, right, (((0,), (0,)), ((), ())), preferred_element_type=jnp.float32
    )


def body(tokens_in, norm_gain, positions, blocks, slot_code, out_grad):
    tok_rows = tokens_in.shape[0]
    feat = tokens_in.shape[1]
    groups = lax.axis_size("wt")
    slab_index = lax.axis_index("seq")
    is_even = lax.axis_index("wt") % 2 == 0
    pos_count = 2 * (D // BLK)
    row_blocks = pos_count // 2
    slot_codes = slot_code[0]
    is_live = slot_codes >= 0
    target_user = jnp.where(is_live, slot_codes // pos_count, 0)
    user_match = (
        (target_user[:, None] == jnp.arange(groups, dtype=jnp.int32)[None, :]) & is_live[:, None]
    ).astype(jnp.int32)
    earlier = jnp.cumsum(user_match, axis=0) - user_match
    slot_rank = jnp.sum(earlier * user_match, axis=1)
    dump_slot = groups * CAP
    slot_dest = jnp.where(is_live, target_user * CAP + slot_rank, dump_slot)
    block_place = (slot_codes - target_user * pos_count).astype(jnp.float32)
    dest_match = slot_dest[:, None] == jnp.arange(dump_slot, dtype=jnp.int32)[None, :]
    dest_source = jnp.sum(
        jnp.where(dest_match, jnp.arange(slot_dest.shape[0], dtype=jnp.int32)[:, None], 0), axis=0
    )
    dest_used = jnp.any(dest_match, axis=0)
    outgoing = jnp.where(dest_used[:, None, None], blocks[0][dest_source], jnp.zeros((), jnp.bfloat16))
    outgoing_pos = (
        jnp.full((dump_slot + 1,), -1.0, jnp.float32)
        .at[slot_dest]
        .set(block_place)
        .astype(jnp.bfloat16)
    )
    arrived, arrived_pos = (
        lax.all_to_all(
            outgoing.reshape(groups, CAP, BLK, BLK),
            "wt",
            split_axis=0,
            concat_axis=0,
            tiled=True,
        ),
        lax.all_to_all(
            outgoing_pos[:dump_slot].reshape(groups, CAP),
            "wt",
            split_axis=0,
            concat_axis=0,
            tiled=True,
        ),
    )
    gain_hi = lax.reduce_precision(norm_gain, exponent_bits=8, mantissa_bits=7)
    gain_rest = norm_gain - gain_hi
    gain_mid = lax.reduce_precision(gain_rest, exponent_bits=8, mantissa_bits=7)
    gain_lo = gain_rest - gain_mid
    gain_rows = jnp.stack([gain_hi, gain_mid, gain_lo]).astype(jnp.bfloat16)
    side_rows = 8
    gathered = lax.all_gather(
        jnp.concatenate(
            [tokens_in, gain_rows, jnp.zeros((side_rows - 3, feat), jnp.bfloat16)], axis=0
        ),
        "wt",
        axis=1,
        tiled=True,
    )
    tokens_full = gathered[:tok_rows]
    gain_parts = gathered[tok_rows : tok_rows + 3].astype(jnp.float32)
    gain_full = (gain_parts[0] + gain_parts[1]) + gain_parts[2]
    full_f32 = tokens_full.astype(jnp.float32)
    squares = jnp.sum(full_f32 * full_f32, axis=1)
    inv_rms = lax.rsqrt(squares / D + norm_eps)
    scaled_full = full_f32 * inv_rms[:, None]
    gained_full = scaled_full * gain_full[None, :]
    normed = gained_full.astype(jnp.bfloat16)
    scaled = tokens_in.astype(jnp.float32) * inv_rms[:, None]
    arrival = arrived_pos.reshape(-1).astype(jnp.int32)
    arrival = jnp.where(arrival < 0, pos_count, arrival)
    place_match = arrival[:, None] == jnp.arange(pos_count, dtype=jnp.int32)[None, :]
    place_source = jnp.sum(
        jnp.where(place_match, jnp.arange(arrival.shape[0], dtype=jnp.int32)[:, None], 0), axis=0
    )
    place_used = jnp.any(place_match, axis=0)
    weight_table = jnp.where(
        place_used[:, None, None],
        arrived.reshape(-1, BLK, BLK)[place_source],
        jnp.zeros((), jnp.bfloat16),
    )
    w_query = weight_table[:row_blocks].reshape(D, HD)
    w_pair = weight_table[row_blocks:pos_count].reshape(D, HD)
    query_proj = jnp.dot(normed, w_query, preferred_element_type=jnp.float32)
    pair_proj = jnp.dot(normed, w_pair, preferred_element_type=jnp.float32)
    cos_table, sin_table = rope_tables(positions, HD)
    query_rot = (rotate(query_proj, cos_table, sin_table) * query_scale).astype(jnp.bfloat16)
    own_pair = jnp.where(is_even, rotate(pair_proj, cos_table, sin_table), pair_proj).astype(
        jnp.bfloat16
    )
    partner = from_partner(own_pair, "wt", 0)
    key_rows = jnp.where(is_even, own_pair, partner)
    value_rows = jnp.where(is_even, partner, own_pair)
    reach_slabs = lax.axis_size("seq") // 2
    window = reach_slabs * tok_rows
    key_value = jnp.concatenate([key_rows, value_rows], axis=1)
    key_list = [key_rows]
    value_list = [value_rows]
    for offset in range(1, reach_slabs + 1):
        prev = shifted(key_value, "seq", offset)
        key_list.append(prev[:, :HD])
        value_list.append(prev[:, HD:])
    key_all = jnp.concatenate(key_list, axis=0)
    value_all = jnp.concatenate(value_list, axis=0)
    local_index = jnp.arange(tok_rows, dtype=jnp.int32)
    query_index = slab_index * tok_rows + local_index
    key_index = jnp.concatenate(
        [(slab_index - offset) * tok_rows + local_index for offset in range(reach_slabs + 1)]
    )
    doc_begin = query_index - positions
    distance = query_index[:, None] - key_index[None, :]
    visible = (distance >= 0) & (distance < window) & (key_index[None, :] >= doc_begin[:, None])
    scores = contract(query_rot, key_all)
    capped = soft_cap * jnp.tanh(scores / soft_cap)
    exp_scores = jnp.where(visible, jnp.exp(capped), 0.0)
    row_total = jnp.sum(exp_scores, axis=1)
    attn_rows = (
        jnp.dot(exp_scores.astype(jnp.bfloat16), value_all, preferred_element_type=jnp.float32)
        / row_total[:, None]
    ).astype(jnp.bfloat16)
    row_delta = jnp.sum(out_grad.astype(jnp.float32) * attn_rows.astype(jnp.float32), axis=1)
    soft_probs = exp_scores / row_total[:, None]
    prob_grad = contract(out_grad, value_all)
    score_grad = soft_probs * (prob_grad - row_delta[:, None]) * (1.0 - (capped / soft_cap) ** 2)
    score_low = score_grad.astype(jnp.bfloat16)
    probs_low = soft_probs.astype(jnp.bfloat16)
    rot_grad = jnp.dot(score_low, key_all, preferred_element_type=jnp.float32)
    query_grad = (rotate(rot_grad, cos_table, -sin_table) * query_scale).astype(jnp.bfloat16)
    key_grads = contract_rows(score_low, query_rot)
    value_grads = contract_rows(probs_low, out_grad)
    key_total = key_grads[:tok_rows]
    value_total = value_grads[:tok_rows]
    for offset in range(1, reach_slabs + 1):
        piece = jnp.concatenate(
            [
                key_grads[offset * tok_rows : (offset + 1) * tok_rows].astype(jnp.bfloat16),
                value_grads[offset * tok_rows : (offset + 1) * tok_rows].astype(jnp.bfloat16),
            ],
            axis=1,
        )
        recv = shifted(piece, "seq", -offset).astype(jnp.float32)
        key_total = key_total + recv[:, :HD]
        value_total = value_total + recv[:, HD:]
    outbound = jnp.where(is_even, value_total, key_total)
    partner_grad = from_partner(outbound.astype(jnp.bfloat16), "wt", 0).astype(outbound.dtype)
    pair_total = jnp.where(is_even, key_total, value_total) + partner_grad
    pair_grad = jnp.where(is_even, rotate(pair_total, cos_table, -sin_table), pair_total).astype(
        jnp.bfloat16
    )
    contribution = contract(w_query, query_grad) + contract(w_pair, pair_grad)
    row_part = jnp.sum(contribution * gained_full.T, axis=0)
    row_top = lax.reduce_precision(row_part, exponent_bits=8, mantissa_bits=7)
    row_hi = row_top.astype(jnp.bfloat16)
    row_lo = (row_part - row_top).astype(jnp.bfloat16)
    pad_rows = 16
    extra_rows = jnp.concatenate(
        [row_hi[None], row_lo[None], jnp.zeros((pad_rows - 2, tok_rows), jnp.bfloat16)], axis=0
    )
    packed = jnp.concatenate(
        [
            contribution.astype(jnp.bfloat16).reshape(groups, feat, tok_rows),
            jnp.broadcast_to(extra_rows[None], (groups, pad_rows, tok_rows)),
        ],
        axis=1,
    ).reshape(groups * (feat + pad_rows), tok_rows)
    scattered = jnp.sum(
        lax.all_to_all(
            packed.reshape(groups, feat + pad_rows, tok_rows),
            "wt",
            split_axis=0,
            concat_axis=0,
            tiled=True,
        ).astype(jnp.float32),
        axis=0,
    )
    normed_grad = scattered[:feat].astype(jnp.float32).T
    row_dots = scattered[feat].astype(jnp.float32) + scattered[feat + 1].astype(jnp.float32)
    scaled_grad = normed_grad * norm_gain[None, :]
    tokens_grad = (inv_rms[:, None] * (scaled_grad - scaled * (row_dots / D)[:, None])).astype(
        jnp.bfloat16
    )
    n_seq = lax.axis_size("seq")
    band = BLK // n_seq
    slots = slot_dest.shape[0]
    band_rows = CAP * band
    block_rows = groups * band_rows
    matrix_rows = row_blocks * band
    side = 16

    def banded(matrix_grad):
        return jnp.transpose(
            matrix_grad.reshape(row_blocks, n_seq, band, BLK), (1, 0, 2, 3)
        ).reshape(n_seq, matrix_rows, BLK)

    grad_query = contract_rows(normed, query_grad)
    query_recv = lax.all_to_all(
        banded(grad_query).astype(jnp.bfloat16), "seq", split_axis=0, concat_axis=0, tiled=True
    )
    query_band = jnp.sum(query_recv.astype(jnp.float32), axis=0)
    grad_pair = contract_rows(normed, pair_grad)
    gain_width = D // n_seq
    per_chunk = gain_width // feat
    head_gain = jnp.sum(contribution * scaled_full.T, axis=1)
    head_top = lax.reduce_precision(head_gain, exponent_bits=8, mantissa_bits=7)
    head_pair = jnp.stack([head_top, head_gain - head_top]).astype(jnp.bfloat16)
    gain_send = jnp.transpose(head_pair.reshape(2, n_seq, gain_width), (1, 0, 2)).reshape(
        n_seq, 2 * gain_width
    )
    gain_send = jnp.pad(gain_send, ((0, 0), (0, side * BLK - 2 * gain_width))).reshape(
        n_seq, side, BLK
    )
    pair_recv = lax.all_to_all(
        jnp.concatenate([banded(grad_pair).astype(jnp.bfloat16), gain_send], axis=1),
        "seq",
        split_axis=0,
        concat_axis=0,
        tiled=True,
    )
    pair_sum = jnp.sum(pair_recv.astype(jnp.float32), axis=0)
    band_table = jnp.concatenate(
        [
            query_band.reshape(row_blocks, band, BLK),
            pair_sum[:matrix_rows].reshape(row_blocks, band, BLK),
            jnp.zeros((1, band, BLK), jnp.float32),
        ],
        axis=0,
    )
    block_chunk = band_table[arrival].astype(jnp.bfloat16).reshape(groups, band_rows, BLK)
    gain_flat = pair_sum[matrix_rows:].reshape(-1)
    gain_chunk = gain_flat[:gain_width] + gain_flat[gain_width : 2 * gain_width]
    chunk_top = lax.reduce_precision(gain_chunk, exponent_bits=8, mantissa_bits=7)
    chunk_pair = jnp.stack([chunk_top, gain_chunk - chunk_top]).astype(jnp.bfloat16)
    chunk_dest = jnp.transpose(chunk_pair.reshape(2, per_chunk, feat), (1, 0, 2)).reshape(
        per_chunk, 2 * feat
    )
    gain_slots = lax.dynamic_update_slice(
        jnp.zeros((groups, side * BLK), jnp.bfloat16), chunk_dest, (slab_index * per_chunk, 0)
    ).reshape(groups, side, BLK)
    wt_recv = lax.all_to_all(
        jnp.concatenate([block_chunk, gain_slots], axis=1),
        "wt",
        split_axis=0,
        concat_axis=0,
        tiled=True,
    )
    returned = wt_recv[:, :band_rows].astype(jnp.float32).reshape(groups * CAP, band, BLK)
    owned_band = jnp.concatenate([returned, jnp.zeros((1, band, BLK), jnp.float32)], axis=0)[
        slot_dest
    ]
    gain_recv = wt_recv[:, band_rows:].reshape(groups, side * BLK)[:, : 2 * feat]
    gain_recv = gain_recv.astype(jnp.float32)
    gain_mine = jnp.sum(gain_recv[:, :feat] + gain_recv[:, feat:], axis=0)
    mine_top = lax.reduce_precision(gain_mine, exponent_bits=8, mantissa_bits=7)
    mine_pair = jnp.stack([mine_top, gain_mine - mine_top]).astype(jnp.bfloat16).reshape(-1)
    owned_rows = slots * band
    gather_send = jnp.concatenate(
        [
            owned_band.reshape(owned_rows, BLK).astype(jnp.bfloat16),
            jnp.pad(mine_pair, (0, side * BLK - 2 * feat)).reshape(side, BLK),
        ],
        axis=0,
    )
    gathered_back = lax.all_gather(gather_send, "seq", axis=0, tiled=True).reshape(
        n_seq, owned_rows + side, BLK
    )
    block_grads = (
        jnp.transpose(
            gathered_back[:, :owned_rows]
            .astype(jnp.float32)
            .reshape(n_seq, slots, band, BLK),
            (1, 0, 2, 3),
        )
        .reshape(slots, BLK, BLK)
        .astype(jnp.bfloat16)
    )
    gain_back = gathered_back[:, owned_rows:].reshape(n_seq, side * BLK).astype(jnp.float32)
    gain_total = jnp.sum(gain_back[:, :feat] + gain_back[:, feat : 2 * feat], axis=0)
    return (attn_rows, tokens_grad, gain_total, block_grads[None])


def solution(mesh):
    placed = (
        P("seq", "wt"),
        P("wt"),
        P("seq"),
        P("wt", None, None, None),
        P("wt", None),
        P("seq", "wt"),
    )
    return jax.shard_map(
        body,
        mesh=mesh,
        in_specs=placed,
        out_specs=(P("seq", "wt"), P("seq", "wt"), P("wt"), P("wt", None, None, None)),
        check_vma=False,
    )
```

```python
import jax
import jax.numpy as jnp
from jax import lax
from jax.sharding import PartitionSpec as P

D = 4608
HD = 128
BLK = 128
CAP = 2


query_scale = 144.0 ** (-0.5)
soft_cap = 50.0
norm_eps = 1e-06


def from_partner(block, axis, stride):
    count = lax.axis_size(axis)
    route = []
    for low in range(count):
        high = low | 1 << stride
        if high != low and high < count:
            route += [(low, high), (high, low)]
    return lax.ppermute(block, axis, route)


def shifted(value, axis, steps):
    count = lax.axis_size(axis)
    initial, last = (max(0, -steps), min(count, count - steps))
    return lax.ppermute(value, axis, [(source, source + steps) for source in range(initial, last)])


def rope_tables(positions, head_width):
    half_width = head_width // 2
    frequency = 10000.0 ** (-2.0 * jnp.arange(half_width, dtype=jnp.float32) / head_width)
    angles = positions.astype(jnp.float32)[:, None] * frequency[None, :]
    return (jnp.cos(angles), jnp.sin(angles))


def rotate(vector, cos_table, sin_table):
    half_width = vector.shape[-1] // 2
    first_half = vector[..., :half_width]
    second_half = vector[..., half_width:]
    return jnp.concatenate(
        [
            first_half * cos_table - second_half * sin_table,
            first_half * sin_table + second_half * cos_table,
        ],
        axis=-1,
    )


def contract(left, right):
    return lax.dot_general(
        left, right, (((1,), (1,)), ((), ())), preferred_element_type=jnp.float32
    )


def contract_rows(left, right):
    return lax.dot_general(
        left, right, (((0,), (0,)), ((), ())), preferred_element_type=jnp.float32
    )


def body(tokens_in, norm_gain, positions, blocks, slot_code, out_grad):
    tok_rows = tokens_in.shape[0]
    feat = tokens_in.shape[1]
    groups = lax.axis_size("wt")
    slab_index = lax.axis_index("seq")
    is_even = lax.axis_index("wt") % 2 == 0
    pos_count = 2 * (D // BLK)
    row_blocks = pos_count // 2
    slot_codes = slot_code[0]
    is_live = slot_codes >= 0
    target_user = jnp.where(is_live, slot_codes // pos_count, 0)
    user_match = (
        (target_user[:, None] == jnp.arange(groups, dtype=jnp.int32)[None, :]) & is_live[:, None]
    ).astype(jnp.int32)
    earlier = jnp.cumsum(user_match, axis=0) - user_match
    slot_rank = jnp.sum(earlier * user_match, axis=1)
    dump_slot = groups * CAP
    slot_dest = jnp.where(is_live, target_user * CAP + slot_rank, dump_slot)
    block_place = (slot_codes - target_user * pos_count).astype(jnp.float32)
    outgoing = jnp.zeros((dump_slot + 1, BLK, BLK), jnp.bfloat16).at[slot_dest].set(blocks[0])
    outgoing_pos = (
        jnp.full((dump_slot + 1,), -1.0, jnp.float32)
        .at[slot_dest]
        .set(block_place)
        .astype(jnp.bfloat16)
    )
    arrived, arrived_pos = (
        lax.all_to_all(
            outgoing[:dump_slot].reshape(groups, CAP, BLK, BLK),
            "wt",
            split_axis=0,
            concat_axis=0,
            tiled=True,
        ),
        lax.all_to_all(
            outgoing_pos[:dump_slot].reshape(groups, CAP),
            "wt",
            split_axis=0,
            concat_axis=0,
            tiled=True,
        ),
    )
    gain_hi = lax.reduce_precision(norm_gain, exponent_bits=8, mantissa_bits=7)
    gain_rest = norm_gain - gain_hi
    gain_mid = lax.reduce_precision(gain_rest, exponent_bits=8, mantissa_bits=7)
    gain_lo = gain_rest - gain_mid
    gain_rows = jnp.stack([gain_hi, gain_mid, gain_lo]).astype(jnp.bfloat16)
    side_rows = 8
    gathered = lax.all_gather(
        jnp.concatenate(
            [tokens_in, gain_rows, jnp.zeros((side_rows - 3, feat), jnp.bfloat16)], axis=0
        ),
        "wt",
        axis=1,
        tiled=True,
    )
    tokens_full = gathered[:tok_rows]
    gain_parts = gathered[tok_rows : tok_rows + 3].astype(jnp.float32)
    gain_full = (gain_parts[0] + gain_parts[1]) + gain_parts[2]
    full_f32 = tokens_full.astype(jnp.float32)
    squares = jnp.sum(full_f32 * full_f32, axis=1)
    inv_rms = lax.rsqrt(squares / D + norm_eps)
    scaled_full = full_f32 * inv_rms[:, None]
    gained_full = scaled_full * gain_full[None, :]
    normed = gained_full.astype(jnp.bfloat16)
    scaled = tokens_in.astype(jnp.float32) * inv_rms[:, None]
    arrival = arrived_pos.reshape(-1).astype(jnp.int32)
    arrival = jnp.where(arrival < 0, pos_count, arrival)
    weight_table = (
        jnp.zeros((pos_count + 1, BLK, BLK), jnp.bfloat16)
        .at[arrival]
        .set(arrived.reshape(-1, BLK, BLK))
    )
    w_query = weight_table[:row_blocks].reshape(D, HD)
    w_pair = weight_table[row_blocks:pos_count].reshape(D, HD)
    query_proj = jnp.dot(normed, w_query, preferred_element_type=jnp.float32)
    pair_proj = jnp.dot(normed, w_pair, preferred_element_type=jnp.float32)
    cos_table, sin_table = rope_tables(positions, HD)
    query_rot = (rotate(query_proj, cos_table, sin_table) * query_scale).astype(jnp.bfloat16)
    own_pair = jnp.where(is_even, rotate(pair_proj, cos_table, sin_table), pair_proj).astype(
        jnp.bfloat16
    )
    reach_slabs = lax.axis_size("seq") // 2
    window = reach_slabs * tok_rows
    own_list = [own_pair]
    for offset in range(1, reach_slabs + 1):
        own_list.append(shifted(own_pair, "seq", offset))
    own_all = jnp.concatenate(own_list, axis=0)
    partner_all = from_partner(own_all, "wt", 0)
    key_all = jnp.where(is_even, own_all, partner_all)
    value_all = jnp.where(is_even, partner_all, own_all)
    local_index = jnp.arange(tok_rows, dtype=jnp.int32)
    query_index = slab_index * tok_rows + local_index
    key_index = jnp.concatenate(
        [(slab_index - offset) * tok_rows + local_index for offset in range(reach_slabs + 1)]
    )
    doc_begin = query_index - positions
    distance = query_index[:, None] - key_index[None, :]
    visible = (distance >= 0) & (distance < window) & (key_index[None, :] >= doc_begin[:, None])
    scores = contract(query_rot, key_all)
    capped = soft_cap * jnp.tanh(scores / soft_cap)
    exp_scores = jnp.where(visible, jnp.exp(capped), 0.0)
    row_total = jnp.sum(exp_scores, axis=1)
    attn_rows = (
        jnp.dot(exp_scores.astype(jnp.bfloat16), value_all, preferred_element_type=jnp.float32)
        / row_total[:, None]
    ).astype(jnp.bfloat16)
    row_delta = jnp.sum(out_grad.astype(jnp.float32) * attn_rows.astype(jnp.float32), axis=1)
    soft_probs = exp_scores / row_total[:, None]
    prob_grad = contract(out_grad, value_all)
    score_grad = soft_probs * (prob_grad - row_delta[:, None]) * (1.0 - (capped / soft_cap) ** 2)
    score_low = score_grad.astype(jnp.bfloat16)
    probs_low = soft_probs.astype(jnp.bfloat16)
    rot_grad = jnp.dot(score_low, key_all, preferred_element_type=jnp.float32)
    query_grad = (rotate(rot_grad, cos_table, -sin_table) * query_scale).astype(jnp.bfloat16)
    key_grads = contract_rows(score_low, query_rot)
    value_grads = contract_rows(probs_low, out_grad)
    outbound = jnp.where(is_even, value_grads, key_grads).astype(jnp.bfloat16)
    partner_grads = from_partner(outbound, "wt", 0).astype(jnp.float32)
    own_grads = jnp.where(is_even, key_grads, value_grads) + partner_grads
    pair_total = own_grads[:tok_rows]
    for offset in range(1, reach_slabs + 1):
        piece = own_grads[offset * tok_rows : (offset + 1) * tok_rows].astype(jnp.bfloat16)
        pair_total = pair_total + shifted(piece, "seq", -offset).astype(jnp.float32)
    pair_grad = jnp.where(is_even, rotate(pair_total, cos_table, -sin_table), pair_total).astype(
        jnp.bfloat16
    )
    contribution = contract(w_query, query_grad) + contract(w_pair, pair_grad)
    row_part = jnp.sum(contribution * gained_full.T, axis=0)
    row_top = lax.reduce_precision(row_part, exponent_bits=8, mantissa_bits=7)
    row_hi = row_top.astype(jnp.bfloat16)
    row_lo = (row_part - row_top).astype(jnp.bfloat16)
    pad_rows = 16
    extra_rows = jnp.concatenate(
        [row_hi[None], row_lo[None], jnp.zeros((pad_rows - 2, tok_rows), jnp.bfloat16)], axis=0
    )
    packed = jnp.concatenate(
        [
            contribution.astype(jnp.bfloat16).reshape(groups, feat, tok_rows),
            jnp.broadcast_to(extra_rows[None], (groups, pad_rows, tok_rows)),
        ],
        axis=1,
    ).reshape(groups * (feat + pad_rows), tok_rows)
    scattered = jnp.sum(
        lax.all_to_all(
            packed.reshape(groups, feat + pad_rows, tok_rows),
            "wt",
            split_axis=0,
            concat_axis=0,
            tiled=True,
        ).astype(jnp.float32),
        axis=0,
    )
    normed_grad = scattered[:feat].astype(jnp.float32).T
    row_dots = scattered[feat].astype(jnp.float32) + scattered[feat + 1].astype(jnp.float32)
    scaled_grad = normed_grad * norm_gain[None, :]
    tokens_grad = (inv_rms[:, None] * (scaled_grad - scaled * (row_dots / D)[:, None])).astype(
        jnp.bfloat16
    )
    grad_query = contract_rows(normed, query_grad)
    grad_pair = contract_rows(normed, pair_grad)
    grad_table = jnp.concatenate(
        [
            grad_query.reshape(row_blocks, BLK, BLK),
            grad_pair.reshape(row_blocks, BLK, BLK),
            jnp.zeros((1, BLK, BLK), jnp.float32),
        ],
        axis=0,
    )
    n_seq = lax.axis_size("seq")
    band = BLK // n_seq
    slots = slot_dest.shape[0]
    band_rows = CAP * band
    block_rows = groups * band_rows
    side = 16
    block_send = jnp.transpose(
        grad_table[arrival].reshape(groups, CAP, n_seq, band, BLK), (2, 0, 1, 3, 4)
    ).reshape(n_seq, block_rows, BLK)
    gain_width = D // n_seq
    per_chunk = gain_width // feat
    head_gain = jnp.sum(contribution * scaled_full.T, axis=1)
    head_top = lax.reduce_precision(head_gain, exponent_bits=8, mantissa_bits=7)
    head_pair = jnp.stack([head_top, head_gain - head_top]).astype(jnp.bfloat16)
    gain_send = jnp.transpose(head_pair.reshape(2, n_seq, gain_width), (1, 0, 2)).reshape(
        n_seq, 2 * gain_width
    )
    gain_send = jnp.pad(gain_send, ((0, 0), (0, side * BLK - 2 * gain_width))).reshape(
        n_seq, side, BLK
    )
    seq_recv = lax.all_to_all(
        jnp.concatenate([block_send.astype(jnp.bfloat16), gain_send], axis=1),
        "seq",
        split_axis=0,
        concat_axis=0,
        tiled=True,
    )
    seq_sum = jnp.sum(seq_recv.astype(jnp.float32), axis=0)
    block_chunk = seq_sum[:block_rows].astype(jnp.bfloat16).reshape(groups, band_rows, BLK)
    gain_flat = seq_sum[block_rows:].reshape(-1)
    gain_chunk = gain_flat[:gain_width] + gain_flat[gain_width : 2 * gain_width]
    chunk_top = lax.reduce_precision(gain_chunk, exponent_bits=8, mantissa_bits=7)
    chunk_pair = jnp.stack([chunk_top, gain_chunk - chunk_top]).astype(jnp.bfloat16)
    chunk_dest = jnp.transpose(chunk_pair.reshape(2, per_chunk, feat), (1, 0, 2)).reshape(
        per_chunk, 2 * feat
    )
    gain_slots = lax.dynamic_update_slice(
        jnp.zeros((groups, side * BLK), jnp.bfloat16), chunk_dest, (slab_index * per_chunk, 0)
    ).reshape(groups, side, BLK)
    wt_recv = lax.all_to_all(
        jnp.concatenate([block_chunk, gain_slots], axis=1),
        "wt",
        split_axis=0,
        concat_axis=0,
        tiled=True,
    )
    returned = wt_recv[:, :band_rows].astype(jnp.float32).reshape(groups * CAP, band, BLK)
    owned_band = jnp.concatenate([returned, jnp.zeros((1, band, BLK), jnp.float32)], axis=0)[
        slot_dest
    ]
    gain_recv = wt_recv[:, band_rows:].reshape(groups, side * BLK)[:, : 2 * feat]
    gain_recv = gain_recv.astype(jnp.float32)
    gain_mine = jnp.sum(gain_recv[:, :feat] + gain_recv[:, feat:], axis=0)
    mine_top = lax.reduce_precision(gain_mine, exponent_bits=8, mantissa_bits=7)
    mine_pair = jnp.stack([mine_top, gain_mine - mine_top]).astype(jnp.bfloat16).reshape(-1)
    owned_rows = slots * band
    gather_send = jnp.concatenate(
        [
            owned_band.reshape(owned_rows, BLK).astype(jnp.bfloat16),
            jnp.pad(mine_pair, (0, side * BLK - 2 * feat)).reshape(side, BLK),
        ],
        axis=0,
    )
    gathered_back = lax.all_gather(gather_send, "seq", axis=0, tiled=True).reshape(
        n_seq, owned_rows + side, BLK
    )
    block_grads = (
        jnp.transpose(
            gathered_back[:, :owned_rows]
            .astype(jnp.float32)
            .reshape(n_seq, slots, band, BLK),
            (1, 0, 2, 3),
        )
        .reshape(slots, BLK, BLK)
        .astype(jnp.bfloat16)
    )
    gain_back = gathered_back[:, owned_rows:].reshape(n_seq, side * BLK).astype(jnp.float32)
    gain_total = jnp.sum(gain_back[:, :feat] + gain_back[:, feat : 2 * feat], axis=0)
    return (attn_rows, tokens_grad, gain_total, block_grads[None])


def solution(mesh):
    placed = (
        P("seq", "wt"),
        P("wt"),
        P("seq"),
        P("wt", None, None, None),
        P("wt", None),
        P("seq", "wt"),
    )
    return jax.shard_map(
        body,
        mesh=mesh,
        in_specs=placed,
        out_specs=(P("seq", "wt"), P("seq", "wt"), P("wt"), P("wt", None, None, None)),
        check_vma=False,
    )
```

```python
import jax
import jax.numpy as jnp
from jax import lax
from jax.sharding import PartitionSpec as P

D = 4608
HD = 128
BLK = 128
CAP = 2


query_scale = 144.0 ** (-0.5)
soft_cap = 50.0
WT = ("chip", "core")
norm_eps = 1e-06


def from_partner(block, axis, stride):
    count = lax.axis_size(axis)
    route = []
    for low in range(count):
        high = low | 1 << stride
        if high != low and high < count:
            route += [(low, high), (high, low)]
    return lax.ppermute(block, axis, route)


def shifted(value, axis, steps):
    count = lax.axis_size(axis)
    initial, last = (max(0, -steps), min(count, count - steps))
    return lax.ppermute(value, axis, [(source, source + steps) for source in range(initial, last)])


def rope_tables(positions, head_width):
    half_width = head_width // 2
    frequency = 10000.0 ** (-2.0 * jnp.arange(half_width, dtype=jnp.float32) / head_width)
    angles = positions.astype(jnp.float32)[:, None] * frequency[None, :]
    return (jnp.cos(angles), jnp.sin(angles))


def rotate(vector, cos_table, sin_table):
    half_width = vector.shape[-1] // 2
    first_half = vector[..., :half_width]
    second_half = vector[..., half_width:]
    return jnp.concatenate(
        [
            first_half * cos_table - second_half * sin_table,
            first_half * sin_table + second_half * cos_table,
        ],
        axis=-1,
    )


def contract(left, right):
    return lax.dot_general(
        left, right, (((1,), (1,)), ((), ())), preferred_element_type=jnp.float32
    )


def contract_rows(left, right):
    return lax.dot_general(
        left, right, (((0,), (0,)), ((), ())), preferred_element_type=jnp.float32
    )


def body(tokens_in, norm_gain, positions, blocks, slot_code, out_grad):
    tok_rows = tokens_in.shape[0]
    feat = tokens_in.shape[1]
    groups = lax.axis_size(WT)
    slab_index = lax.axis_index("seq")
    is_even = lax.axis_index(WT) % 2 == 0
    pos_count = 2 * (D // BLK)
    row_blocks = pos_count // 2
    slot_codes = slot_code[0]
    is_live = slot_codes >= 0
    target_user = jnp.where(is_live, slot_codes // pos_count, 0)
    user_match = (
        (target_user[:, None] == jnp.arange(groups, dtype=jnp.int32)[None, :]) & is_live[:, None]
    ).astype(jnp.int32)
    earlier = jnp.cumsum(user_match, axis=0) - user_match
    slot_rank = jnp.sum(earlier * user_match, axis=1)
    dump_slot = groups * CAP
    slot_dest = jnp.where(is_live, target_user * CAP + slot_rank, dump_slot)
    block_place = (slot_codes - target_user * pos_count).astype(jnp.float32)
    outgoing = jnp.zeros((dump_slot + 1, BLK, BLK), jnp.bfloat16).at[slot_dest].set(blocks[0])
    outgoing_pos = (
        jnp.full((dump_slot + 1,), -1.0, jnp.float32)
        .at[slot_dest]
        .set(block_place)
        .astype(jnp.bfloat16)
    )
    arrived, arrived_pos = (
        lax.all_to_all(
            outgoing[:dump_slot].reshape(groups, CAP, BLK, BLK),
            WT,
            split_axis=0,
            concat_axis=0,
            tiled=True,
        ),
        lax.all_to_all(
            outgoing_pos[:dump_slot].reshape(groups, CAP),
            WT,
            split_axis=0,
            concat_axis=0,
            tiled=True,
        ),
    )
    gain_hi = lax.reduce_precision(norm_gain, exponent_bits=8, mantissa_bits=7)
    gain_rest = norm_gain - gain_hi
    gain_mid = lax.reduce_precision(gain_rest, exponent_bits=8, mantissa_bits=7)
    gain_lo = gain_rest - gain_mid
    gain_rows = jnp.stack([gain_hi, gain_mid, gain_lo]).astype(jnp.bfloat16)
    side_rows = 8
    half = lax.all_gather(
        jnp.concatenate(
            [tokens_in, gain_rows, jnp.zeros((side_rows - 3, feat), jnp.bfloat16)], axis=0
        ),
        "chip",
        axis=1,
        tiled=True,
    )
    other_half = from_partner(half, "core", 0)
    first_core = lax.axis_index("core") == 0
    chips = lax.axis_size("chip")
    gathered = jnp.stack(
        [
            jnp.where(first_core, half, other_half).reshape(-1, chips, feat),
            jnp.where(first_core, other_half, half).reshape(-1, chips, feat),
        ],
        axis=2,
    ).reshape(-1, chips * 2 * feat)
    tokens_full = gathered[:tok_rows]
    gain_parts = gathered[tok_rows : tok_rows + 3].astype(jnp.float32)
    gain_full = (gain_parts[0] + gain_parts[1]) + gain_parts[2]
    full_f32 = tokens_full.astype(jnp.float32)
    squares = jnp.sum(full_f32 * full_f32, axis=1)
    inv_rms = lax.rsqrt(squares / D + norm_eps)
    scaled_full = full_f32 * inv_rms[:, None]
    gained_full = scaled_full * gain_full[None, :]
    normed = gained_full.astype(jnp.bfloat16)
    scaled = tokens_in.astype(jnp.float32) * inv_rms[:, None]
    arrival = arrived_pos.reshape(-1).astype(jnp.int32)
    arrival = jnp.where(arrival < 0, pos_count, arrival)
    weight_table = (
        jnp.zeros((pos_count + 1, BLK, BLK), jnp.bfloat16)
        .at[arrival]
        .set(arrived.reshape(-1, BLK, BLK))
    )
    w_query = weight_table[:row_blocks].reshape(D, HD)
    w_pair = weight_table[row_blocks:pos_count].reshape(D, HD)
    query_proj = jnp.dot(normed, w_query, preferred_element_type=jnp.float32)
    pair_proj = jnp.dot(normed, w_pair, preferred_element_type=jnp.float32)
    cos_table, sin_table = rope_tables(positions, HD)
    query_rot = (rotate(query_proj, cos_table, sin_table) * query_scale).astype(jnp.bfloat16)
    own_pair = jnp.where(is_even, rotate(pair_proj, cos_table, sin_table), pair_proj).astype(
        jnp.bfloat16
    )
    reach_slabs = lax.axis_size("seq") // 2
    window = reach_slabs * tok_rows
    own_list = [own_pair]
    for offset in range(1, reach_slabs + 1):
        own_list.append(shifted(own_pair, "seq", offset))
    own_all = jnp.concatenate(own_list, axis=0)
    partner_all = from_partner(own_all, "core", 0)
    key_all = jnp.where(is_even, own_all, partner_all)
    value_all = jnp.where(is_even, partner_all, own_all)
    local_index = jnp.arange(tok_rows, dtype=jnp.int32)
    query_index = slab_index * tok_rows + local_index
    key_index = jnp.concatenate(
        [(slab_index - offset) * tok_rows + local_index for offset in range(reach_slabs + 1)]
    )
    doc_begin = query_index - positions
    distance = query_index[:, None] - key_index[None, :]
    visible = (distance >= 0) & (distance < window) & (key_index[None, :] >= doc_begin[:, None])
    scores = contract(query_rot, key_all)
    capped = soft_cap * jnp.tanh(scores / soft_cap)
    exp_scores = jnp.where(visible, jnp.exp(capped), 0.0)
    row_total = jnp.sum(exp_scores, axis=1)
    attn_rows = (
        jnp.dot(exp_scores.astype(jnp.bfloat16), value_all, preferred_element_type=jnp.float32)
        / row_total[:, None]
    ).astype(jnp.bfloat16)
    row_delta = jnp.sum(out_grad.astype(jnp.float32) * attn_rows.astype(jnp.float32), axis=1)
    soft_probs = exp_scores / row_total[:, None]
    prob_grad = contract(out_grad, value_all)
    score_grad = soft_probs * (prob_grad - row_delta[:, None]) * (1.0 - (capped / soft_cap) ** 2)
    score_low = score_grad.astype(jnp.bfloat16)
    probs_low = soft_probs.astype(jnp.bfloat16)
    rot_grad = jnp.dot(score_low, key_all, preferred_element_type=jnp.float32)
    query_grad = (rotate(rot_grad, cos_table, -sin_table) * query_scale).astype(jnp.bfloat16)
    key_grads = contract_rows(score_low, query_rot)
    value_grads = contract_rows(probs_low, out_grad)
    outbound = jnp.where(is_even, value_grads, key_grads).astype(jnp.bfloat16)
    partner_grads = from_partner(outbound, "core", 0).astype(jnp.float32)
    own_grads = jnp.where(is_even, key_grads, value_grads) + partner_grads
    pair_total = own_grads[:tok_rows]
    for offset in range(1, reach_slabs + 1):
        piece = own_grads[offset * tok_rows : (offset + 1) * tok_rows].astype(jnp.bfloat16)
        pair_total = pair_total + shifted(piece, "seq", -offset).astype(jnp.float32)
    pair_grad = jnp.where(is_even, rotate(pair_total, cos_table, -sin_table), pair_total).astype(
        jnp.bfloat16
    )
    contribution = contract(w_query, query_grad) + contract(w_pair, pair_grad)
    row_part = jnp.sum(contribution * gained_full.T, axis=0)
    row_top = lax.reduce_precision(row_part, exponent_bits=8, mantissa_bits=7)
    row_hi = row_top.astype(jnp.bfloat16)
    row_lo = (row_part - row_top).astype(jnp.bfloat16)
    pad_rows = 16
    extra_rows = jnp.concatenate(
        [row_hi[None], row_lo[None], jnp.zeros((pad_rows - 2, tok_rows), jnp.bfloat16)], axis=0
    )
    packed = jnp.concatenate(
        [
            contribution.astype(jnp.bfloat16).reshape(groups, feat, tok_rows),
            jnp.broadcast_to(extra_rows[None], (groups, pad_rows, tok_rows)),
        ],
        axis=1,
    ).reshape(groups * (feat + pad_rows), tok_rows)
    scattered = jnp.sum(
        lax.all_to_all(
            packed.reshape(groups, feat + pad_rows, tok_rows),
            WT,
            split_axis=0,
            concat_axis=0,
            tiled=True,
        ).astype(jnp.float32),
        axis=0,
    )
    normed_grad = scattered[:feat].astype(jnp.float32).T
    row_dots = scattered[feat].astype(jnp.float32) + scattered[feat + 1].astype(jnp.float32)
    scaled_grad = normed_grad * norm_gain[None, :]
    tokens_grad = (inv_rms[:, None] * (scaled_grad - scaled * (row_dots / D)[:, None])).astype(
        jnp.bfloat16
    )
    grad_query = contract_rows(normed, query_grad)
    grad_pair = contract_rows(normed, pair_grad)
    grad_table = jnp.concatenate(
        [
            grad_query.reshape(row_blocks, BLK, BLK),
            grad_pair.reshape(row_blocks, BLK, BLK),
            jnp.zeros((1, BLK, BLK), jnp.float32),
        ],
        axis=0,
    )
    n_seq = lax.axis_size("seq")
    band = BLK // n_seq
    slots = slot_dest.shape[0]
    band_rows = CAP * band
    block_rows = groups * band_rows
    side = 16
    block_send = jnp.transpose(
        grad_table[arrival].reshape(groups, CAP, n_seq, band, BLK), (2, 0, 1, 3, 4)
    ).reshape(n_seq, block_rows, BLK)
    gain_width = D // n_seq
    per_chunk = gain_width // feat
    head_gain = jnp.sum(contribution * scaled_full.T, axis=1)
    head_top = lax.reduce_precision(head_gain, exponent_bits=8, mantissa_bits=7)
    head_pair = jnp.stack([head_top, head_gain - head_top]).astype(jnp.bfloat16)
    gain_send = jnp.transpose(head_pair.reshape(2, n_seq, gain_width), (1, 0, 2)).reshape(
        n_seq, 2 * gain_width
    )
    gain_send = jnp.pad(gain_send, ((0, 0), (0, side * BLK - 2 * gain_width))).reshape(
        n_seq, side, BLK
    )
    seq_recv = lax.all_to_all(
        jnp.concatenate([block_send.astype(jnp.bfloat16), gain_send], axis=1),
        "seq",
        split_axis=0,
        concat_axis=0,
        tiled=True,
    )
    seq_sum = jnp.sum(seq_recv.astype(jnp.float32), axis=0)
    block_chunk = seq_sum[:block_rows].astype(jnp.bfloat16).reshape(groups, band_rows, BLK)
    gain_flat = seq_sum[block_rows:].reshape(-1)
    gain_chunk = gain_flat[:gain_width] + gain_flat[gain_width : 2 * gain_width]
    chunk_top = lax.reduce_precision(gain_chunk, exponent_bits=8, mantissa_bits=7)
    chunk_pair = jnp.stack([chunk_top, gain_chunk - chunk_top]).astype(jnp.bfloat16)
    chunk_dest = jnp.transpose(chunk_pair.reshape(2, per_chunk, feat), (1, 0, 2)).reshape(
        per_chunk, 2 * feat
    )
    gain_slots = lax.dynamic_update_slice(
        jnp.zeros((groups, side * BLK), jnp.bfloat16), chunk_dest, (slab_index * per_chunk, 0)
    ).reshape(groups, side, BLK)
    wt_recv = lax.all_to_all(
        jnp.concatenate([block_chunk, gain_slots], axis=1),
        WT,
        split_axis=0,
        concat_axis=0,
        tiled=True,
    )
    returned = wt_recv[:, :band_rows].astype(jnp.float32).reshape(groups * CAP, band, BLK)
    owned_band = jnp.concatenate([returned, jnp.zeros((1, band, BLK), jnp.float32)], axis=0)[
        slot_dest
    ]
    gain_recv = wt_recv[:, band_rows:].reshape(groups, side * BLK)[:, : 2 * feat]
    gain_recv = gain_recv.astype(jnp.float32)
    gain_mine = jnp.sum(gain_recv[:, :feat] + gain_recv[:, feat:], axis=0)
    mine_top = lax.reduce_precision(gain_mine, exponent_bits=8, mantissa_bits=7)
    mine_pair = jnp.stack([mine_top, gain_mine - mine_top]).astype(jnp.bfloat16).reshape(-1)
    owned_rows = slots * band
    gather_send = jnp.concatenate(
        [
            owned_band.reshape(owned_rows, BLK).astype(jnp.bfloat16),
            jnp.pad(mine_pair, (0, side * BLK - 2 * feat)).reshape(side, BLK),
        ],
        axis=0,
    )
    gathered_back = lax.all_gather(gather_send, "seq", axis=0, tiled=True).reshape(
        n_seq, owned_rows + side, BLK
    )
    block_grads = (
        jnp.transpose(
            gathered_back[:, :owned_rows]
            .astype(jnp.float32)
            .reshape(n_seq, slots, band, BLK),
            (1, 0, 2, 3),
        )
        .reshape(slots, BLK, BLK)
        .astype(jnp.bfloat16)
    )
    gain_back = gathered_back[:, owned_rows:].reshape(n_seq, side * BLK).astype(jnp.float32)
    gain_total = jnp.sum(gain_back[:, :feat] + gain_back[:, feat : 2 * feat], axis=0)
    return (attn_rows, tokens_grad, gain_total, block_grads[None])


def solution(mesh):
    seq_count, wt_count = mesh.devices.shape
    split_mesh = jax.sharding.Mesh(
        mesh.devices.reshape(seq_count, wt_count // 2, 2), ("seq", "chip", "core")
    )
    placed = (
        P("seq", WT),
        P(WT),
        P("seq"),
        P(WT, None, None, None),
        P(WT, None),
        P("seq", WT),
    )
    return jax.shard_map(
        body,
        mesh=split_mesh,
        in_specs=placed,
        out_specs=(P("seq", WT), P("seq", WT), P(WT), P(WT, None, None, None)),
        check_vma=False,
    )
```

```python
import jax
import jax.numpy as jnp
from jax import lax
from jax.sharding import PartitionSpec as P

D = 4608
HD = 128
BLK = 128
CAP = 2


query_scale = 144.0 ** (-0.5)
soft_cap = 50.0
norm_eps = 1e-06


def from_partner(block, axis, stride):
    count = lax.axis_size(axis)
    route = []
    for low in range(count):
        high = low | 1 << stride
        if high != low and high < count:
            route += [(low, high), (high, low)]
    return lax.ppermute(block, axis, route)


def shifted(value, axis, steps):
    count = lax.axis_size(axis)
    initial, last = (max(0, -steps), min(count, count - steps))
    return lax.ppermute(value, axis, [(source, source + steps) for source in range(initial, last)])


def rope_tables(positions, head_width):
    half_width = head_width // 2
    frequency = 10000.0 ** (-2.0 * jnp.arange(half_width, dtype=jnp.float32) / head_width)
    angles = positions.astype(jnp.float32)[:, None] * frequency[None, :]
    return (jnp.cos(angles), jnp.sin(angles))


def rotate(vector, cos_table, sin_table):
    half_width = vector.shape[-1] // 2
    first_half = vector[..., :half_width]
    second_half = vector[..., half_width:]
    return jnp.concatenate(
        [
            first_half * cos_table - second_half * sin_table,
            first_half * sin_table + second_half * cos_table,
        ],
        axis=-1,
    )


def contract(left, right):
    return lax.dot_general(
        left, right, (((1,), (1,)), ((), ())), preferred_element_type=jnp.float32
    )


def contract_rows(left, right):
    return lax.dot_general(
        left, right, (((0,), (0,)), ((), ())), preferred_element_type=jnp.float32
    )


def body(tokens_in, norm_gain, positions, blocks, slot_code, out_grad):
    tok_rows = tokens_in.shape[0]
    feat = tokens_in.shape[1]
    groups = lax.axis_size("wt")
    slab_index = lax.axis_index("seq")
    is_even = lax.axis_index("wt") % 2 == 0
    pos_count = 2 * (D // BLK)
    row_blocks = pos_count // 2
    slot_codes = slot_code[0]
    is_live = slot_codes >= 0
    target_user = jnp.where(is_live, slot_codes // pos_count, 0)
    user_match = (
        (target_user[:, None] == jnp.arange(groups, dtype=jnp.int32)[None, :]) & is_live[:, None]
    ).astype(jnp.int32)
    earlier = jnp.cumsum(user_match, axis=0) - user_match
    slot_rank = jnp.sum(earlier * user_match, axis=1)
    dump_slot = groups * CAP
    slot_dest = jnp.where(is_live, target_user * CAP + slot_rank, dump_slot)
    block_place = (slot_codes - target_user * pos_count).astype(jnp.float32)
    dest_match = slot_dest[:, None] == jnp.arange(dump_slot, dtype=jnp.int32)[None, :]
    dest_source = jnp.sum(
        jnp.where(dest_match, jnp.arange(slot_dest.shape[0], dtype=jnp.int32)[:, None], 0), axis=0
    )
    dest_used = jnp.any(dest_match, axis=0)
    outgoing = jnp.where(dest_used[:, None, None], blocks[0][dest_source], jnp.zeros((), jnp.bfloat16))
    outgoing_pos = (
        jnp.full((dump_slot + 1,), -1.0, jnp.float32)
        .at[slot_dest]
        .set(block_place)
        .astype(jnp.bfloat16)
    )
    arrived, arrived_pos = (
        lax.all_to_all(
            outgoing.reshape(groups, CAP, BLK, BLK),
            "wt",
            split_axis=0,
            concat_axis=0,
            tiled=True,
        ),
        lax.all_to_all(
            outgoing_pos[:dump_slot].reshape(groups, CAP),
            "wt",
            split_axis=0,
            concat_axis=0,
            tiled=True,
        ),
    )
    gain_hi = lax.reduce_precision(norm_gain, exponent_bits=8, mantissa_bits=7)
    gain_rest = norm_gain - gain_hi
    gain_mid = lax.reduce_precision(gain_rest, exponent_bits=8, mantissa_bits=7)
    gain_lo = gain_rest - gain_mid
    gain_rows = jnp.stack([gain_hi, gain_mid, gain_lo]).astype(jnp.bfloat16)
    side_rows = 8
    gathered = lax.all_gather(
        jnp.concatenate(
            [tokens_in, gain_rows, jnp.zeros((side_rows - 3, feat), jnp.bfloat16)], axis=0
        ),
        "wt",
        axis=1,
        tiled=True,
    )
    tokens_full = gathered[:tok_rows]
    gain_parts = gathered[tok_rows : tok_rows + 3].astype(jnp.float32)
    gain_full = (gain_parts[0] + gain_parts[1]) + gain_parts[2]
    full_f32 = tokens_full.astype(jnp.float32)
    squares = jnp.sum(full_f32 * full_f32, axis=1)
    inv_rms = lax.rsqrt(squares / D + norm_eps)
    scaled_full = full_f32 * inv_rms[:, None]
    gained_full = scaled_full * gain_full[None, :]
    normed = gained_full.astype(jnp.bfloat16)
    scaled = tokens_in.astype(jnp.float32) * inv_rms[:, None]
    arrival = arrived_pos.reshape(-1).astype(jnp.int32)
    arrival = jnp.where(arrival < 0, pos_count, arrival)
    place_match = arrival[:, None] == jnp.arange(pos_count, dtype=jnp.int32)[None, :]
    place_source = jnp.sum(
        jnp.where(place_match, jnp.arange(arrival.shape[0], dtype=jnp.int32)[:, None], 0), axis=0
    )
    place_used = jnp.any(place_match, axis=0)
    weight_table = jnp.where(
        place_used[:, None, None],
        arrived.reshape(-1, BLK, BLK)[place_source],
        jnp.zeros((), jnp.bfloat16),
    )
    w_query = weight_table[:row_blocks].reshape(D, HD)
    w_pair = weight_table[row_blocks:pos_count].reshape(D, HD)
    query_proj = jnp.dot(normed, w_query, preferred_element_type=jnp.float32)
    pair_proj = jnp.dot(normed, w_pair, preferred_element_type=jnp.float32)
    cos_table, sin_table = rope_tables(positions, HD)
    query_rot = (rotate(query_proj, cos_table, sin_table) * query_scale).astype(jnp.bfloat16)
    own_pair = jnp.where(is_even, rotate(pair_proj, cos_table, sin_table), pair_proj).astype(
        jnp.bfloat16
    )
    reach_slabs = lax.axis_size("seq") // 2
    window = reach_slabs * tok_rows
    own_list = [own_pair]
    for offset in range(1, reach_slabs + 1):
        own_list.append(shifted(own_pair, "seq", offset))
    own_all = jnp.concatenate(own_list, axis=0)
    partner_all = from_partner(own_all, "wt", 0)
    key_all = jnp.where(is_even, own_all, partner_all)
    value_all = jnp.where(is_even, partner_all, own_all)
    local_index = jnp.arange(tok_rows, dtype=jnp.int32)
    query_index = slab_index * tok_rows + local_index
    key_index = jnp.concatenate(
        [(slab_index - offset) * tok_rows + local_index for offset in range(reach_slabs + 1)]
    )
    doc_begin = query_index - positions
    distance = query_index[:, None] - key_index[None, :]
    visible = (distance >= 0) & (distance < window) & (key_index[None, :] >= doc_begin[:, None])
    scores = contract(query_rot, key_all)
    capped = soft_cap * jnp.tanh(scores / soft_cap)
    exp_scores = jnp.where(visible, jnp.exp(capped), 0.0)
    row_total = jnp.sum(exp_scores, axis=1)
    attn_rows = (
        jnp.dot(exp_scores.astype(jnp.bfloat16), value_all, preferred_element_type=jnp.float32)
        / row_total[:, None]
    ).astype(jnp.bfloat16)
    row_delta = jnp.sum(out_grad.astype(jnp.float32) * attn_rows.astype(jnp.float32), axis=1)
    soft_probs = exp_scores / row_total[:, None]
    prob_grad = contract(out_grad, value_all)
    score_grad = soft_probs * (prob_grad - row_delta[:, None]) * (1.0 - (capped / soft_cap) ** 2)
    score_low = score_grad.astype(jnp.bfloat16)
    probs_low = soft_probs.astype(jnp.bfloat16)
    rot_grad = jnp.dot(score_low, key_all, preferred_element_type=jnp.float32)
    query_grad = (rotate(rot_grad, cos_table, -sin_table) * query_scale).astype(jnp.bfloat16)
    key_grads = contract_rows(score_low, query_rot)
    value_grads = contract_rows(probs_low, out_grad)
    outbound = jnp.where(is_even, value_grads, key_grads).astype(jnp.bfloat16)
    partner_grads = from_partner(outbound, "wt", 0).astype(jnp.float32)
    own_grads = jnp.where(is_even, key_grads, value_grads) + partner_grads
    pair_total = own_grads[:tok_rows]
    for offset in range(1, reach_slabs + 1):
        piece = own_grads[offset * tok_rows : (offset + 1) * tok_rows].astype(jnp.bfloat16)
        pair_total = pair_total + shifted(piece, "seq", -offset).astype(jnp.float32)
    pair_grad = jnp.where(is_even, rotate(pair_total, cos_table, -sin_table), pair_total).astype(
        jnp.bfloat16
    )
    contribution = contract(w_query, query_grad) + contract(w_pair, pair_grad)
    row_part = jnp.sum(contribution * gained_full.T, axis=0)
    row_top = lax.reduce_precision(row_part, exponent_bits=8, mantissa_bits=7)
    row_hi = row_top.astype(jnp.bfloat16)
    row_lo = (row_part - row_top).astype(jnp.bfloat16)
    scattered = jnp.sum(
        lax.all_to_all(
            contribution.astype(jnp.bfloat16).reshape(groups, feat, tok_rows),
            "wt",
            split_axis=0,
            concat_axis=0,
            tiled=True,
        ).astype(jnp.float32),
        axis=0,
    )
    normed_grad = scattered.T
    grad_query = contract_rows(normed, query_grad)
    grad_pair = contract_rows(normed, pair_grad)
    grad_table = jnp.concatenate(
        [
            grad_query.reshape(row_blocks, BLK, BLK),
            grad_pair.reshape(row_blocks, BLK, BLK),
            jnp.zeros((1, BLK, BLK), jnp.float32),
        ],
        axis=0,
    )
    n_seq = lax.axis_size("seq")
    band = BLK // n_seq
    slots = slot_dest.shape[0]
    band_rows = CAP * band
    block_rows = groups * band_rows
    side = 16
    block_send = jnp.transpose(
        grad_table[arrival].reshape(groups, CAP, n_seq, band, BLK), (2, 0, 1, 3, 4)
    ).reshape(n_seq, block_rows, BLK)
    gain_width = D // n_seq
    per_chunk = gain_width // feat
    head_gain = jnp.sum(contribution * scaled_full.T, axis=1)
    head_top = lax.reduce_precision(head_gain, exponent_bits=8, mantissa_bits=7)
    head_pair = jnp.stack([head_top, head_gain - head_top]).astype(jnp.bfloat16)
    gain_send = jnp.transpose(head_pair.reshape(2, n_seq, gain_width), (1, 0, 2)).reshape(
        n_seq, 2 * gain_width
    )
    gain_send = jnp.pad(gain_send, ((0, 0), (0, side * BLK - 2 * gain_width))).reshape(
        n_seq, side, BLK
    )
    seq_recv = lax.all_to_all(
        jnp.concatenate([block_send.astype(jnp.bfloat16), gain_send], axis=1),
        "seq",
        split_axis=0,
        concat_axis=0,
        tiled=True,
    )
    seq_sum = jnp.sum(seq_recv.astype(jnp.float32), axis=0)
    block_chunk = seq_sum[:block_rows].astype(jnp.bfloat16).reshape(groups, band_rows, BLK)
    gain_flat = seq_sum[block_rows:].reshape(-1)
    gain_chunk = gain_flat[:gain_width] + gain_flat[gain_width : 2 * gain_width]
    chunk_top = lax.reduce_precision(gain_chunk, exponent_bits=8, mantissa_bits=7)
    chunk_pair = jnp.stack([chunk_top, gain_chunk - chunk_top]).astype(jnp.bfloat16)
    chunk_dest = jnp.transpose(chunk_pair.reshape(2, per_chunk, feat), (1, 0, 2)).reshape(
        per_chunk, 2 * feat
    )
    row_cols = jnp.concatenate([row_hi, row_lo])
    gain_slots = jnp.concatenate(
        [
            lax.dynamic_update_slice(
                jnp.zeros((groups, 2 * feat), jnp.bfloat16), chunk_dest, (slab_index * per_chunk, 0)
            ),
            jnp.broadcast_to(row_cols[None], (groups, 2 * tok_rows)),
            jnp.zeros((groups, side * BLK - 2 * feat - 2 * tok_rows), jnp.bfloat16),
        ],
        axis=1,
    ).reshape(groups, side, BLK)
    wt_recv = lax.all_to_all(
        jnp.concatenate([block_chunk, gain_slots], axis=1),
        "wt",
        split_axis=0,
        concat_axis=0,
        tiled=True,
    )
    returned = wt_recv[:, :band_rows].astype(jnp.float32).reshape(groups * CAP, band, BLK)
    owned_band = jnp.concatenate([returned, jnp.zeros((1, band, BLK), jnp.float32)], axis=0)[
        slot_dest
    ]
    slot_recv = wt_recv[:, band_rows:].reshape(groups, side * BLK)
    gain_recv = slot_recv[:, : 2 * feat].astype(jnp.float32)
    row_recv = slot_recv[:, 2 * feat : 2 * feat + 2 * tok_rows].astype(jnp.float32)
    row_dots = jnp.sum(row_recv[:, :tok_rows] + row_recv[:, tok_rows:], axis=0)
    scaled_grad = normed_grad * norm_gain[None, :]
    tokens_grad = (inv_rms[:, None] * (scaled_grad - scaled * (row_dots / D)[:, None])).astype(
        jnp.bfloat16
    )
    gain_mine = jnp.sum(gain_recv[:, :feat] + gain_recv[:, feat:], axis=0)
    mine_top = lax.reduce_precision(gain_mine, exponent_bits=8, mantissa_bits=7)
    mine_pair = jnp.stack([mine_top, gain_mine - mine_top]).astype(jnp.bfloat16).reshape(-1)
    owned_rows = slots * band
    gather_send = jnp.concatenate(
        [
            owned_band.reshape(owned_rows, BLK).astype(jnp.bfloat16),
            jnp.pad(mine_pair, (0, side * BLK - 2 * feat)).reshape(side, BLK),
        ],
        axis=0,
    )
    gathered_back = lax.all_gather(gather_send, "seq", axis=0, tiled=True).reshape(
        n_seq, owned_rows + side, BLK
    )
    block_grads = (
        jnp.transpose(
            gathered_back[:, :owned_rows]
            .astype(jnp.float32)
            .reshape(n_seq, slots, band, BLK),
            (1, 0, 2, 3),
        )
        .reshape(slots, BLK, BLK)
        .astype(jnp.bfloat16)
    )
    gain_back = gathered_back[:, owned_rows:].reshape(n_seq, side * BLK).astype(jnp.float32)
    gain_total = jnp.sum(gain_back[:, :feat] + gain_back[:, feat : 2 * feat], axis=0)
    return (attn_rows, tokens_grad, gain_total, block_grads[None])


def solution(mesh):
    placed = (
        P("seq", "wt"),
        P("wt"),
        P("seq"),
        P("wt", None, None, None),
        P("wt", None),
        P("seq", "wt"),
    )
    return jax.shard_map(
        body,
        mesh=mesh,
        in_specs=placed,
        out_specs=(P("seq", "wt"), P("seq", "wt"), P("wt"), P("wt", None, None, None)),
        check_vma=False,
    )
```

```python
import jax
import jax.numpy as jnp
from jax import lax
from jax.sharding import PartitionSpec as P

D = 4608
HD = 128
BLK = 128
CAP = 2


query_scale = 144.0 ** (-0.5)
soft_cap = 50.0
WT = ("chip", "core")
norm_eps = 1e-06


def from_partner(block, axis, stride):
    count = lax.axis_size(axis)
    route = []
    for low in range(count):
        high = low | 1 << stride
        if high != low and high < count:
            route += [(low, high), (high, low)]
    return lax.ppermute(block, axis, route)


def shifted(value, axis, steps):
    count = lax.axis_size(axis)
    initial, last = (max(0, -steps), min(count, count - steps))
    return lax.ppermute(value, axis, [(source, source + steps) for source in range(initial, last)])


def rope_tables(positions, head_width):
    half_width = head_width // 2
    frequency = 10000.0 ** (-2.0 * jnp.arange(half_width, dtype=jnp.float32) / head_width)
    angles = positions.astype(jnp.float32)[:, None] * frequency[None, :]
    return (jnp.cos(angles), jnp.sin(angles))


def rotate(vector, cos_table, sin_table):
    half_width = vector.shape[-1] // 2
    first_half = vector[..., :half_width]
    second_half = vector[..., half_width:]
    return jnp.concatenate(
        [
            first_half * cos_table - second_half * sin_table,
            first_half * sin_table + second_half * cos_table,
        ],
        axis=-1,
    )


def contract(left, right):
    return lax.dot_general(
        left, right, (((1,), (1,)), ((), ())), preferred_element_type=jnp.float32
    )


def contract_rows(left, right):
    return lax.dot_general(
        left, right, (((0,), (0,)), ((), ())), preferred_element_type=jnp.float32
    )


def body(tokens_in, norm_gain, positions, blocks, slot_code, out_grad):
    tok_rows = tokens_in.shape[0]
    feat = tokens_in.shape[1]
    groups = lax.axis_size(WT)
    slab_index = lax.axis_index("seq")
    is_even = lax.axis_index(WT) % 2 == 0
    pos_count = 2 * (D // BLK)
    row_blocks = pos_count // 2
    slot_codes = slot_code[0]
    is_live = slot_codes >= 0
    target_user = jnp.where(is_live, slot_codes // pos_count, 0)
    user_match = (
        (target_user[:, None] == jnp.arange(groups, dtype=jnp.int32)[None, :]) & is_live[:, None]
    ).astype(jnp.int32)
    earlier = jnp.cumsum(user_match, axis=0) - user_match
    slot_rank = jnp.sum(earlier * user_match, axis=1)
    dump_slot = groups * CAP
    slot_dest = jnp.where(is_live, target_user * CAP + slot_rank, dump_slot)
    block_place = (slot_codes - target_user * pos_count).astype(jnp.float32)
    dest_match = slot_dest[:, None] == jnp.arange(dump_slot, dtype=jnp.int32)[None, :]
    dest_source = jnp.sum(
        jnp.where(dest_match, jnp.arange(slot_dest.shape[0], dtype=jnp.int32)[:, None], 0), axis=0
    )
    dest_used = jnp.any(dest_match, axis=0)
    outgoing = jnp.where(dest_used[:, None, None], blocks[0][dest_source], jnp.zeros((), jnp.bfloat16))
    outgoing_pos = (
        jnp.full((dump_slot + 1,), -1.0, jnp.float32)
        .at[slot_dest]
        .set(block_place)
        .astype(jnp.bfloat16)
    )
    arrived, arrived_pos = (
        lax.all_to_all(
            outgoing.reshape(groups, CAP, BLK, BLK),
            WT,
            split_axis=0,
            concat_axis=0,
            tiled=True,
        ),
        lax.all_to_all(
            outgoing_pos[:dump_slot].reshape(groups, CAP),
            WT,
            split_axis=0,
            concat_axis=0,
            tiled=True,
        ),
    )
    gain_hi = lax.reduce_precision(norm_gain, exponent_bits=8, mantissa_bits=7)
    gain_rest = norm_gain - gain_hi
    gain_mid = lax.reduce_precision(gain_rest, exponent_bits=8, mantissa_bits=7)
    gain_lo = gain_rest - gain_mid
    gain_rows = jnp.stack([gain_hi, gain_mid, gain_lo]).astype(jnp.bfloat16)
    side_rows = 8
    gathered = lax.all_gather(
        jnp.concatenate(
            [tokens_in, gain_rows, jnp.zeros((side_rows - 3, feat), jnp.bfloat16)], axis=0
        ),
        WT,
        axis=1,
        tiled=True,
    )
    tokens_full = gathered[:tok_rows]
    gain_parts = gathered[tok_rows : tok_rows + 3].astype(jnp.float32)
    gain_full = (gain_parts[0] + gain_parts[1]) + gain_parts[2]
    full_f32 = tokens_full.astype(jnp.float32)
    squares = jnp.sum(full_f32 * full_f32, axis=1)
    inv_rms = lax.rsqrt(squares / D + norm_eps)
    scaled_full = full_f32 * inv_rms[:, None]
    gained_full = scaled_full * gain_full[None, :]
    normed = gained_full.astype(jnp.bfloat16)
    scaled = tokens_in.astype(jnp.float32) * inv_rms[:, None]
    arrival = arrived_pos.reshape(-1).astype(jnp.int32)
    arrival = jnp.where(arrival < 0, pos_count, arrival)
    place_match = arrival[:, None] == jnp.arange(pos_count, dtype=jnp.int32)[None, :]
    place_source = jnp.sum(
        jnp.where(place_match, jnp.arange(arrival.shape[0], dtype=jnp.int32)[:, None], 0), axis=0
    )
    place_used = jnp.any(place_match, axis=0)
    weight_table = jnp.where(
        place_used[:, None, None],
        arrived.reshape(-1, BLK, BLK)[place_source],
        jnp.zeros((), jnp.bfloat16),
    )
    w_query = weight_table[:row_blocks].reshape(D, HD)
    w_pair = weight_table[row_blocks:pos_count].reshape(D, HD)
    query_proj = jnp.dot(normed, w_query, preferred_element_type=jnp.float32)
    pair_proj = jnp.dot(normed, w_pair, preferred_element_type=jnp.float32)
    cos_table, sin_table = rope_tables(positions, HD)
    query_rot = (rotate(query_proj, cos_table, sin_table) * query_scale).astype(jnp.bfloat16)
    own_pair = jnp.where(is_even, rotate(pair_proj, cos_table, sin_table), pair_proj).astype(
        jnp.bfloat16
    )
    reach_slabs = lax.axis_size("seq") // 2
    window = reach_slabs * tok_rows
    own_list = [own_pair]
    for offset in range(1, reach_slabs + 1):
        own_list.append(shifted(own_pair, "seq", offset))
    own_all = jnp.concatenate(own_list, axis=0)
    partner_all = from_partner(own_all, "core", 0)
    key_all = jnp.where(is_even, own_all, partner_all)
    value_all = jnp.where(is_even, partner_all, own_all)
    local_index = jnp.arange(tok_rows, dtype=jnp.int32)
    query_index = slab_index * tok_rows + local_index
    key_index = jnp.concatenate(
        [(slab_index - offset) * tok_rows + local_index for offset in range(reach_slabs + 1)]
    )
    doc_begin = query_index - positions
    distance = query_index[:, None] - key_index[None, :]
    visible = (distance >= 0) & (distance < window) & (key_index[None, :] >= doc_begin[:, None])
    scores = contract(query_rot, key_all)
    capped = soft_cap * jnp.tanh(scores / soft_cap)
    exp_scores = jnp.where(visible, jnp.exp(capped), 0.0)
    row_total = jnp.sum(exp_scores, axis=1)
    attn_rows = (
        jnp.dot(exp_scores.astype(jnp.bfloat16), value_all, preferred_element_type=jnp.float32)
        / row_total[:, None]
    ).astype(jnp.bfloat16)
    row_delta = jnp.sum(out_grad.astype(jnp.float32) * attn_rows.astype(jnp.float32), axis=1)
    soft_probs = exp_scores / row_total[:, None]
    prob_grad = contract(out_grad, value_all)
    score_grad = soft_probs * (prob_grad - row_delta[:, None]) * (1.0 - (capped / soft_cap) ** 2)
    score_low = score_grad.astype(jnp.bfloat16)
    probs_low = soft_probs.astype(jnp.bfloat16)
    rot_grad = jnp.dot(score_low, key_all, preferred_element_type=jnp.float32)
    query_grad = (rotate(rot_grad, cos_table, -sin_table) * query_scale).astype(jnp.bfloat16)
    key_grads = contract_rows(score_low, query_rot)
    value_grads = contract_rows(probs_low, out_grad)
    outbound = jnp.where(is_even, value_grads, key_grads).astype(jnp.bfloat16)
    partner_grads = from_partner(outbound, "core", 0).astype(jnp.float32)
    own_grads = jnp.where(is_even, key_grads, value_grads) + partner_grads
    pair_total = own_grads[:tok_rows]
    for offset in range(1, reach_slabs + 1):
        piece = own_grads[offset * tok_rows : (offset + 1) * tok_rows].astype(jnp.bfloat16)
        pair_total = pair_total + shifted(piece, "seq", -offset).astype(jnp.float32)
    pair_grad = jnp.where(is_even, rotate(pair_total, cos_table, -sin_table), pair_total).astype(
        jnp.bfloat16
    )
    contribution = contract(w_query, query_grad) + contract(w_pair, pair_grad)
    row_part = jnp.sum(contribution * gained_full.T, axis=0)
    row_top = lax.reduce_precision(row_part, exponent_bits=8, mantissa_bits=7)
    row_hi = row_top.astype(jnp.bfloat16)
    row_lo = (row_part - row_top).astype(jnp.bfloat16)
    chips = lax.axis_size("chip")
    core_index = lax.axis_index("core")
    by_core = contribution.reshape(chips, 2, feat, tok_rows)
    keep = lax.dynamic_index_in_dim(by_core, core_index, axis=1, keepdims=False)
    give = lax.dynamic_index_in_dim(by_core, 1 - core_index, axis=1, keepdims=False)
    from_other = from_partner(give.astype(jnp.bfloat16), "core", 0).astype(jnp.float32)
    scattered = jnp.sum(
        lax.all_to_all(
            (keep + from_other).astype(jnp.bfloat16),
            "chip",
            split_axis=0,
            concat_axis=0,
            tiled=True,
        ).astype(jnp.float32),
        axis=0,
    )
    normed_grad = scattered.T
    grad_query = contract_rows(normed, query_grad)
    grad_pair = contract_rows(normed, pair_grad)
    grad_table = jnp.concatenate(
        [
            grad_query.reshape(row_blocks, BLK, BLK),
            grad_pair.reshape(row_blocks, BLK, BLK),
            jnp.zeros((1, BLK, BLK), jnp.float32),
        ],
        axis=0,
    )
    n_seq = lax.axis_size("seq")
    band = BLK // n_seq
    slots = slot_dest.shape[0]
    band_rows = CAP * band
    block_rows = groups * band_rows
    side = 16
    block_send = jnp.transpose(
        grad_table[arrival].reshape(groups, CAP, n_seq, band, BLK), (2, 0, 1, 3, 4)
    ).reshape(n_seq, block_rows, BLK)
    gain_width = D // n_seq
    per_chunk = gain_width // feat
    head_gain = jnp.sum(contribution * scaled_full.T, axis=1)
    head_top = lax.reduce_precision(head_gain, exponent_bits=8, mantissa_bits=7)
    head_pair = jnp.stack([head_top, head_gain - head_top]).astype(jnp.bfloat16)
    gain_send = jnp.transpose(head_pair.reshape(2, n_seq, gain_width), (1, 0, 2)).reshape(
        n_seq, 2 * gain_width
    )
    gain_send = jnp.pad(gain_send, ((0, 0), (0, side * BLK - 2 * gain_width))).reshape(
        n_seq, side, BLK
    )
    seq_recv = lax.all_to_all(
        jnp.concatenate([block_send.astype(jnp.bfloat16), gain_send], axis=1),
        "seq",
        split_axis=0,
        concat_axis=0,
        tiled=True,
    )
    seq_sum = jnp.sum(seq_recv.astype(jnp.float32), axis=0)
    block_chunk = seq_sum[:block_rows].astype(jnp.bfloat16).reshape(groups, band_rows, BLK)
    gain_flat = seq_sum[block_rows:].reshape(-1)
    gain_chunk = gain_flat[:gain_width] + gain_flat[gain_width : 2 * gain_width]
    chunk_top = lax.reduce_precision(gain_chunk, exponent_bits=8, mantissa_bits=7)
    chunk_pair = jnp.stack([chunk_top, gain_chunk - chunk_top]).astype(jnp.bfloat16)
    chunk_dest = jnp.transpose(chunk_pair.reshape(2, per_chunk, feat), (1, 0, 2)).reshape(
        per_chunk, 2 * feat
    )
    row_cols = jnp.concatenate([row_hi, row_lo])
    gain_slots = jnp.concatenate(
        [
            lax.dynamic_update_slice(
                jnp.zeros((groups, 2 * feat), jnp.bfloat16), chunk_dest, (slab_index * per_chunk, 0)
            ),
            jnp.broadcast_to(row_cols[None], (groups, 2 * tok_rows)),
            jnp.zeros((groups, side * BLK - 2 * feat - 2 * tok_rows), jnp.bfloat16),
        ],
        axis=1,
    ).reshape(groups, side, BLK)
    wt_recv = lax.all_to_all(
        jnp.concatenate([block_chunk, gain_slots], axis=1),
        WT,
        split_axis=0,
        concat_axis=0,
        tiled=True,
    )
    returned = wt_recv[:, :band_rows].astype(jnp.float32).reshape(groups * CAP, band, BLK)
    owned_band = jnp.concatenate([returned, jnp.zeros((1, band, BLK), jnp.float32)], axis=0)[
        slot_dest
    ]
    slot_recv = wt_recv[:, band_rows:].reshape(groups, side * BLK)
    gain_recv = slot_recv[:, : 2 * feat].astype(jnp.float32)
    row_recv = slot_recv[:, 2 * feat : 2 * feat + 2 * tok_rows].astype(jnp.float32)
    row_dots = jnp.sum(row_recv[:, :tok_rows] + row_recv[:, tok_rows:], axis=0)
    scaled_grad = normed_grad * norm_gain[None, :]
    tokens_grad = (inv_rms[:, None] * (scaled_grad - scaled * (row_dots / D)[:, None])).astype(
        jnp.bfloat16
    )
    gain_mine = jnp.sum(gain_recv[:, :feat] + gain_recv[:, feat:], axis=0)
    mine_top = lax.reduce_precision(gain_mine, exponent_bits=8, mantissa_bits=7)
    mine_pair = jnp.stack([mine_top, gain_mine - mine_top]).astype(jnp.bfloat16).reshape(-1)
    owned_rows = slots * band
    gather_send = jnp.concatenate(
        [
            owned_band.reshape(owned_rows, BLK).astype(jnp.bfloat16),
            jnp.pad(mine_pair, (0, side * BLK - 2 * feat)).reshape(side, BLK),
        ],
        axis=0,
    )
    gathered_back = lax.all_gather(gather_send, "seq", axis=0, tiled=True).reshape(
        n_seq, owned_rows + side, BLK
    )
    block_grads = (
        jnp.transpose(
            gathered_back[:, :owned_rows]
            .astype(jnp.float32)
            .reshape(n_seq, slots, band, BLK),
            (1, 0, 2, 3),
        )
        .reshape(slots, BLK, BLK)
        .astype(jnp.bfloat16)
    )
    gain_back = gathered_back[:, owned_rows:].reshape(n_seq, side * BLK).astype(jnp.float32)
    gain_total = jnp.sum(gain_back[:, :feat] + gain_back[:, feat : 2 * feat], axis=0)
    return (attn_rows, tokens_grad, gain_total, block_grads[None])


def solution(mesh):
    seq_count, wt_count = mesh.devices.shape
    split_mesh = jax.sharding.Mesh(
        mesh.devices.reshape(seq_count, wt_count // 2, 2), ("seq", "chip", "core")
    )
    placed = (
        P("seq", WT),
        P(WT),
        P("seq"),
        P(WT, None, None, None),
        P(WT, None),
        P("seq", WT),
    )
    return jax.shard_map(
        body,
        mesh=split_mesh,
        in_specs=placed,
        out_specs=(P("seq", WT), P("seq", WT), P(WT), P(WT, None, None, None)),
        check_vma=False,
    )
```

```python
import jax
import jax.numpy as jnp
from jax import lax
from jax.sharding import PartitionSpec as P

D = 4608
HD = 128
BLK = 128
CAP = 2


query_scale = 144.0 ** (-0.5)
soft_cap = 50.0
WT = ("chip", "core")
norm_eps = 1e-06


def from_partner(block, axis, stride):
    count = lax.axis_size(axis)
    route = []
    for low in range(count):
        high = low | 1 << stride
        if high != low and high < count:
            route += [(low, high), (high, low)]
    return lax.ppermute(block, axis, route)


def shifted(value, axis, steps):
    count = lax.axis_size(axis)
    initial, last = (max(0, -steps), min(count, count - steps))
    return lax.ppermute(value, axis, [(source, source + steps) for source in range(initial, last)])


def rope_tables(positions, head_width):
    half_width = head_width // 2
    frequency = 10000.0 ** (-2.0 * jnp.arange(half_width, dtype=jnp.float32) / head_width)
    angles = positions.astype(jnp.float32)[:, None] * frequency[None, :]
    return (jnp.cos(angles), jnp.sin(angles))


def rotate(vector, cos_table, sin_table):
    half_width = vector.shape[-1] // 2
    first_half = vector[..., :half_width]
    second_half = vector[..., half_width:]
    return jnp.concatenate(
        [
            first_half * cos_table - second_half * sin_table,
            first_half * sin_table + second_half * cos_table,
        ],
        axis=-1,
    )


def contract(left, right):
    return lax.dot_general(
        left, right, (((1,), (1,)), ((), ())), preferred_element_type=jnp.float32
    )


def contract_rows(left, right):
    return lax.dot_general(
        left, right, (((0,), (0,)), ((), ())), preferred_element_type=jnp.float32
    )


def body(tokens_in, norm_gain, positions, blocks, slot_code, out_grad):
    tok_rows = tokens_in.shape[0]
    feat = tokens_in.shape[1]
    groups = lax.axis_size(WT)
    slab_index = lax.axis_index("seq")
    is_even = lax.axis_index(WT) % 2 == 0
    pos_count = 2 * (D // BLK)
    row_blocks = pos_count // 2
    slot_codes = slot_code[0]
    is_live = slot_codes >= 0
    target_user = jnp.where(is_live, slot_codes // pos_count, 0)
    user_match = (
        (target_user[:, None] == jnp.arange(groups, dtype=jnp.int32)[None, :]) & is_live[:, None]
    ).astype(jnp.int32)
    earlier = jnp.cumsum(user_match, axis=0) - user_match
    slot_rank = jnp.sum(earlier * user_match, axis=1)
    dump_slot = groups * CAP
    slot_dest = jnp.where(is_live, target_user * CAP + slot_rank, dump_slot)
    block_place = (slot_codes - target_user * pos_count).astype(jnp.float32)
    dest_match = slot_dest[:, None] == jnp.arange(dump_slot, dtype=jnp.int32)[None, :]
    dest_source = jnp.sum(
        jnp.where(dest_match, jnp.arange(slot_dest.shape[0], dtype=jnp.int32)[:, None], 0), axis=0
    )
    dest_used = jnp.any(dest_match, axis=0)
    outgoing = jnp.where(dest_used[:, None, None], blocks[0][dest_source], jnp.zeros((), jnp.bfloat16))
    outgoing_pos = (
        jnp.full((dump_slot + 1,), -1.0, jnp.float32)
        .at[slot_dest]
        .set(block_place)
        .astype(jnp.bfloat16)
    )
    arrived, arrived_pos = (
        lax.all_to_all(
            outgoing.reshape(groups, CAP, BLK, BLK),
            WT,
            split_axis=0,
            concat_axis=0,
            tiled=True,
        ),
        lax.all_to_all(
            outgoing_pos[:dump_slot].reshape(groups, CAP),
            WT,
            split_axis=0,
            concat_axis=0,
            tiled=True,
        ),
    )
    gain_hi = lax.reduce_precision(norm_gain, exponent_bits=8, mantissa_bits=7)
    gain_rest = norm_gain - gain_hi
    gain_mid = lax.reduce_precision(gain_rest, exponent_bits=8, mantissa_bits=7)
    gain_lo = gain_rest - gain_mid
    gain_rows = jnp.stack([gain_hi, gain_mid, gain_lo]).astype(jnp.bfloat16)
    side_rows = 8
    gathered = lax.all_gather(
        jnp.concatenate(
            [tokens_in, gain_rows, jnp.zeros((side_rows - 3, feat), jnp.bfloat16)], axis=0
        ),
        WT,
        axis=1,
        tiled=True,
    )
    tokens_full = gathered[:tok_rows]
    gain_parts = gathered[tok_rows : tok_rows + 3].astype(jnp.float32)
    gain_full = (gain_parts[0] + gain_parts[1]) + gain_parts[2]
    full_f32 = tokens_full.astype(jnp.float32)
    squares = jnp.sum(full_f32 * full_f32, axis=1)
    inv_rms = lax.rsqrt(squares / D + norm_eps)
    scaled_full = full_f32 * inv_rms[:, None]
    gained_full = scaled_full * gain_full[None, :]
    normed = gained_full.astype(jnp.bfloat16)
    scaled = tokens_in.astype(jnp.float32) * inv_rms[:, None]
    arrival = arrived_pos.reshape(-1).astype(jnp.int32)
    arrival = jnp.where(arrival < 0, pos_count, arrival)
    place_match = arrival[:, None] == jnp.arange(pos_count, dtype=jnp.int32)[None, :]
    place_source = jnp.sum(
        jnp.where(place_match, jnp.arange(arrival.shape[0], dtype=jnp.int32)[:, None], 0), axis=0
    )
    place_used = jnp.any(place_match, axis=0)
    weight_table = jnp.where(
        place_used[:, None, None],
        arrived.reshape(-1, BLK, BLK)[place_source],
        jnp.zeros((), jnp.bfloat16),
    )
    w_query = weight_table[:row_blocks].reshape(D, HD)
    w_pair = weight_table[row_blocks:pos_count].reshape(D, HD)
    query_proj = jnp.dot(normed, w_query, preferred_element_type=jnp.float32)
    pair_proj = jnp.dot(normed, w_pair, preferred_element_type=jnp.float32)
    cos_table, sin_table = rope_tables(positions, HD)
    query_rot = (rotate(query_proj, cos_table, sin_table) * query_scale).astype(jnp.bfloat16)
    own_pair = jnp.where(is_even, rotate(pair_proj, cos_table, sin_table), pair_proj).astype(
        jnp.bfloat16
    )
    reach_slabs = lax.axis_size("seq") // 2
    window = reach_slabs * tok_rows
    own_list = [own_pair]
    for offset in range(1, reach_slabs + 1):
        own_list.append(shifted(own_pair, "seq", offset))
    own_all = jnp.concatenate(own_list, axis=0)
    partner_all = from_partner(own_all, "core", 0)
    key_all = jnp.where(is_even, own_all, partner_all)
    value_all = jnp.where(is_even, partner_all, own_all)
    local_index = jnp.arange(tok_rows, dtype=jnp.int32)
    query_index = slab_index * tok_rows + local_index
    key_index = jnp.concatenate(
        [(slab_index - offset) * tok_rows + local_index for offset in range(reach_slabs + 1)]
    )
    doc_begin = query_index - positions
    distance = query_index[:, None] - key_index[None, :]
    visible = (distance >= 0) & (distance < window) & (key_index[None, :] >= doc_begin[:, None])
    scores = contract(query_rot, key_all)
    capped = soft_cap * jnp.tanh(scores / soft_cap)
    exp_scores = jnp.where(visible, jnp.exp(capped), 0.0)
    row_total = jnp.sum(exp_scores, axis=1)
    attn_rows = (
        jnp.dot(exp_scores.astype(jnp.bfloat16), value_all, preferred_element_type=jnp.float32)
        / row_total[:, None]
    ).astype(jnp.bfloat16)
    row_delta = jnp.sum(out_grad.astype(jnp.float32) * attn_rows.astype(jnp.float32), axis=1)
    soft_probs = exp_scores / row_total[:, None]
    prob_grad = contract(out_grad, value_all)
    score_grad = soft_probs * (prob_grad - row_delta[:, None]) * (1.0 - (capped / soft_cap) ** 2)
    score_low = score_grad.astype(jnp.bfloat16)
    probs_low = soft_probs.astype(jnp.bfloat16)
    rot_grad = jnp.dot(score_low, key_all, preferred_element_type=jnp.float32)
    query_grad = (rotate(rot_grad, cos_table, -sin_table) * query_scale).astype(jnp.bfloat16)
    key_grads = contract_rows(score_low, query_rot)
    value_grads = contract_rows(probs_low, out_grad)
    outbound = jnp.where(is_even, value_grads, key_grads).astype(jnp.bfloat16)
    partner_grads = from_partner(outbound, "core", 0).astype(jnp.float32)
    own_grads = jnp.where(is_even, key_grads, value_grads) + partner_grads
    pair_total = own_grads[:tok_rows]
    for offset in range(1, reach_slabs + 1):
        piece = own_grads[offset * tok_rows : (offset + 1) * tok_rows].astype(jnp.bfloat16)
        pair_total = pair_total + shifted(piece, "seq", -offset).astype(jnp.float32)
    pair_grad = jnp.where(is_even, rotate(pair_total, cos_table, -sin_table), pair_total).astype(
        jnp.bfloat16
    )
    contribution = contract(w_query, query_grad) + contract(w_pair, pair_grad)
    row_part = jnp.sum(contribution * gained_full.T, axis=0)
    row_top = lax.reduce_precision(row_part, exponent_bits=8, mantissa_bits=7)
    row_hi = row_top.astype(jnp.bfloat16)
    row_lo = (row_part - row_top).astype(jnp.bfloat16)
    chips = lax.axis_size("chip")
    core_index = lax.axis_index("core")
    by_core = contribution.reshape(chips, 2, feat, tok_rows)
    keep = lax.dynamic_index_in_dim(by_core, core_index, axis=1, keepdims=False)
    give = lax.dynamic_index_in_dim(by_core, 1 - core_index, axis=1, keepdims=False)
    from_other = from_partner(give.astype(jnp.bfloat16), "core", 0).astype(jnp.float32)
    scattered = jnp.sum(
        lax.all_to_all(
            (keep + from_other).astype(jnp.bfloat16),
            "chip",
            split_axis=0,
            concat_axis=0,
            tiled=True,
        ).astype(jnp.float32),
        axis=0,
    )
    normed_grad = scattered.T
    grad_query = contract_rows(normed, query_grad)
    grad_pair = contract_rows(normed, pair_grad)
    grad_table = jnp.concatenate(
        [
            grad_query.reshape(row_blocks, BLK, BLK),
            grad_pair.reshape(row_blocks, BLK, BLK),
            jnp.zeros((1, BLK, BLK), jnp.float32),
        ],
        axis=0,
    )
    n_seq = lax.axis_size("seq")
    band = BLK // n_seq
    slots = slot_dest.shape[0]
    band_rows = CAP * band
    block_rows = groups * band_rows
    side = 16
    block_send = jnp.transpose(
        grad_table[arrival].reshape(groups, CAP, n_seq, band, BLK), (2, 0, 1, 3, 4)
    ).reshape(n_seq, block_rows, BLK)
    gain_width = D // n_seq
    per_chunk = gain_width // feat
    head_gain = jnp.sum(contribution * scaled_full.T, axis=1)
    head_top = lax.reduce_precision(head_gain, exponent_bits=8, mantissa_bits=7)
    head_pair = jnp.stack([head_top, head_gain - head_top]).astype(jnp.bfloat16)
    gain_send = jnp.transpose(head_pair.reshape(2, n_seq, gain_width), (1, 0, 2)).reshape(
        n_seq, 2 * gain_width
    )
    gain_send = jnp.pad(gain_send, ((0, 0), (0, side * BLK - 2 * gain_width))).reshape(
        n_seq, side, BLK
    )
    seq_recv = lax.all_to_all(
        jnp.concatenate([block_send.astype(jnp.bfloat16), gain_send], axis=1),
        "seq",
        split_axis=0,
        concat_axis=0,
        tiled=True,
    )
    seq_sum = jnp.sum(seq_recv.astype(jnp.float32), axis=0)
    block_chunk = seq_sum[:block_rows].astype(jnp.bfloat16).reshape(groups, band_rows, BLK)
    gain_flat = seq_sum[block_rows:].reshape(-1)
    gain_chunk = gain_flat[:gain_width] + gain_flat[gain_width : 2 * gain_width]
    chunk_top = lax.reduce_precision(gain_chunk, exponent_bits=8, mantissa_bits=7)
    chunk_pair = jnp.stack([chunk_top, gain_chunk - chunk_top]).astype(jnp.bfloat16)
    chunk_dest = jnp.transpose(chunk_pair.reshape(2, per_chunk, feat), (1, 0, 2)).reshape(
        per_chunk, 2 * feat
    )
    row_cols = jnp.concatenate([row_hi, row_lo])
    gain_slots = jnp.concatenate(
        [
            lax.dynamic_update_slice(
                jnp.zeros((groups, 2 * feat), jnp.bfloat16), chunk_dest, (slab_index * per_chunk, 0)
            ),
            jnp.broadcast_to(row_cols[None], (groups, 2 * tok_rows)),
            jnp.zeros((groups, side * BLK - 2 * feat - 2 * tok_rows), jnp.bfloat16),
        ],
        axis=1,
    ).reshape(groups, side, BLK)
    wt_recv = lax.all_to_all(
        jnp.concatenate([block_chunk, gain_slots], axis=1),
        WT,
        split_axis=0,
        concat_axis=0,
        tiled=True,
    )
    returned = wt_recv[:, :band_rows].astype(jnp.float32).reshape(groups * CAP, band, BLK)
    owned_band = jnp.concatenate([returned, jnp.zeros((1, band, BLK), jnp.float32)], axis=0)[
        slot_dest
    ]
    slot_recv = wt_recv[:, band_rows:].reshape(groups, side * BLK)
    gain_recv = slot_recv[:, : 2 * feat].astype(jnp.float32)
    row_recv = slot_recv[:, 2 * feat : 2 * feat + 2 * tok_rows].astype(jnp.float32)
    row_dots = jnp.sum(row_recv[:, :tok_rows] + row_recv[:, tok_rows:], axis=0)
    scaled_grad = normed_grad * norm_gain[None, :]
    tokens_grad = (inv_rms[:, None] * (scaled_grad - scaled * (row_dots / D)[:, None])).astype(
        jnp.bfloat16
    )
    gain_mine = jnp.sum(gain_recv[:, :feat] + gain_recv[:, feat:], axis=0)
    mine_top = lax.reduce_precision(gain_mine, exponent_bits=8, mantissa_bits=7)
    mine_pair = jnp.stack([mine_top, gain_mine - mine_top]).astype(jnp.bfloat16).reshape(-1)
    gathered_back = lax.all_gather(
        jnp.concatenate(
            [
                owned_band.astype(jnp.bfloat16),
                jnp.pad(mine_pair, (0, band * BLK - 2 * feat)).reshape(1, band, BLK),
            ],
            axis=0,
        ),
        "seq",
        axis=1,
        tiled=True,
    )
    block_grads = gathered_back[:slots]
    gain_back = gathered_back[slots].reshape(n_seq, band * BLK).astype(jnp.float32)
    gain_total = jnp.sum(gain_back[:, :feat] + gain_back[:, feat : 2 * feat], axis=0)
    return (attn_rows, tokens_grad, gain_total, block_grads[None])


def solution(mesh):
    seq_count, wt_count = mesh.devices.shape
    split_mesh = jax.sharding.Mesh(
        mesh.devices.reshape(seq_count, wt_count // 2, 2), ("seq", "chip", "core")
    )
    placed = (
        P("seq", WT),
        P(WT),
        P("seq"),
        P(WT, None, None, None),
        P(WT, None),
        P("seq", WT),
    )
    return jax.shard_map(
        body,
        mesh=split_mesh,
        in_specs=placed,
        out_specs=(P("seq", WT), P("seq", WT), P(WT), P(WT, None, None, None)),
        check_vma=False,
    )
```
